512 devices in a mesh: sub: 128 (over z_hi, x, y, core), scen: 4 (over z_lo).
Axes of the slice: x: 4, y: 8, z: 8 (z_hi: 2, z_lo: 4; z = z_hi * 4 + z_lo), core: 2. Of those that a mesh axis runs over, the one named last changes fastest.
Arguments:
- inverse_matrix: bfloat16 [128, 1024, 1024], P('sub'), may hold values from -1 to 1
- objective_grad: bfloat16 [48, 128, 64, 1024], P(None, 'sub', 'scen'), may hold values from -6 to 6
- final_adjoint: float32 [128, 64, 1024], P('sub', 'scen'), may hold values from -6 to 6
- companion: float32 [128, 1024], P('sub'), may hold values from 0.95 to 0.995
- port_node: int32 [128, 4, 8], P('sub'), may hold values from 0 to 1023
- line_count: int32 [128, 4], P('sub'), may hold values from 1 to 8, as said below
- line_delay: int32 [128, 4, 8], P('sub'), may hold values from 24 to 47, as said below
- line_admittance: float32 [128, 4, 8], P('sub'), may hold values from 0.3 to 1.2
- later_history: float32 [128, 4, 8, 48, 64], P('sub', None, None, None, 'scen'), may hold values from -6 to 6
- conv_node: int32 [128, 16], P('sub'), may hold values from 0 to 1023
- conv_drive: float32 [128, 48, 64, 16], P('sub', None, 'scen'), may hold values from -0.25 to 0.25
- fault_bus: int32 [64], P('scen'), may hold values from 0 to 131071
- fault_current: float32 [48, 64], P(None, 'scen'), may hold values from -12 to 12
- fault_voltage: float32 [48, 64], P(None, 'scen'), may hold values from -2 to 2
Outputs:
- adjoint_start: float32 [128, 64, 1024], P('sub', 'scen')
- earlier_history: float32 [128, 4, 8, 48, 64], P('sub', None, None, None, 'scen')
- control_sens: float32 [128, 16], P('sub')
- fault_sens: float32 [64], P('scen')
The draws below stay inside these ranges and needn't reach their ends.
Inputs may be any that keep to these rules, and one draw needn't show every extreme that they name: line_count[p, e] equals line_count of the partner subnetwork in the opposite direction; the most is reached in every draw. `line_delay`: both ends of a line have the same delay; both ends of the range are reached in every draw.
All inputs are finite; a program needn't handle non-finite values.
Results may differ from the reference program's by a relative error of at most 0.0088.
Values sent between devices are 32-bit elements; how exact they have to be, the bound alone decides.
No kernel may reach another device: no remote copies, remote signals or barrier semaphores. Data moves between devices by JAX's collectives and lax.ppermute only.
A program may use at most 64 MiB of HBM per device.

```python
import math
import jax
import jax.numpy as jnp
from jax import lax

NODES = 1024
BLOCK = 24
BLOCKS = 2
CAP = 8
CONV = 16
SUBS = 128
SCEN = 64
STEPS = 48
GRIDW = 8


def link_tables(key):
    base_key = jax.random.fold_in(key, 11)
    subkeys = jax.random.split(base_key, 3)
    link_load = jnp.minimum(jax.random.randint(subkeys[0], (2, SUBS), 1, CAP + 1), jax.random.randint(subkeys[1], (2, SUBS), 1, CAP + 1))
    link_load = link_load.at[0, 0].set(CAP)
    link_delay = jax.random.randint(subkeys[2], (2, SUBS, CAP), BLOCK, 2 * BLOCK)
    link_delay = link_delay.at[0, 0, 0].set(2 * BLOCK - 1).at[1, 0, 0].set(BLOCK)
    count_table = jnp.stack([link_load[0], jnp.roll(link_load[0], 1), link_load[1], jnp.roll(link_load[1], GRIDW)], axis=1)
    delay_table = jnp.stack([link_delay[0], jnp.roll(link_delay[0], 1, axis=0), link_delay[1], jnp.roll(link_delay[1], GRIDW, axis=0)], axis=1)
    return (count_table.astype(jnp.int32), delay_table.astype(jnp.int32))


def draw_line_count(key, part):
    return link_tables(key)[0]


def draw_line_delay(key, part):
    return link_tables(key)[1]


def draw_inverse_matrix(key, part):
    noise_key, diag_key = jax.random.split(jax.random.fold_in(key, 3))
    spread = jax.random.normal(noise_key, (SUBS, NODES, NODES), jnp.float32)
    diag_part = jax.random.uniform(diag_key, (SUBS, NODES), jnp.float32, 0.95, 0.98)
    matrix = 0.015 * spread / math.sqrt(NODES) + diag_part[:, :, None] * jnp.eye(NODES, dtype=jnp.float32)[None]
    return matrix.astype(jnp.bfloat16)


def place_ends(result, key, smallest, top_value):
    longest = result.shape.index(max(result.shape))
    spots = []
    for shift in (0, 1):
        where = [jax.random.randint(jax.random.fold_in(key, axis), (), 0, length) for axis, length in enumerate(result.shape)]
        where[longest] = (where[longest] + shift) % result.shape[longest]
        spots.append(tuple(where))
    return result.at[spots[0]].set(smallest).at[spots[1]].set(top_value)


def level_of(stream_key, shape, cuts, smallest, high):
    loudness = 1.0
    for position, parts in cuts:
        heights = jax.random.uniform(jax.random.fold_in(jax.random.fold_in(stream_key, 6), position), (parts,), jnp.float32, smallest / len(cuts), high / len(cuts))
        loudness = loudness * jnp.repeat(jnp.exp(heights), shape[position] // parts).reshape((-1,) + (1,) * (len(shape) - 1 - position))
    return loudness


def bell_draw(stream_key, dims, width, reach, shards=(), held_as=jnp.bfloat16):
    entries = width * jax.random.normal(stream_key, dims, jnp.float32)
    if shards:
        entries = entries * level_of(stream_key, dims, shards, -0.22, 0.18)
    return jnp.clip(entries, -reach, reach).astype(held_as)


def setup_inputs(seed: int = 0) -> dict:
    seeds = jax.random.split(jax.random.key(seed), 15)
    inverse_matrix = draw_inverse_matrix(jax.random.fold_in(seeds[14], 71), 0)
    objective_grad = bell_draw(seeds[1], (STEPS, SUBS, SCEN, NODES), 1.0, 6.0, ((1, 128), (2, 4)))
    final_adjoint = bell_draw(seeds[2], (SUBS, SCEN, NODES), 1.0, 6.0, ((0, 128), (1, 4)), jnp.float32)
    companion = jnp.clip(0.95 + 0.045000017 * jax.random.uniform(seeds[3], (SUBS, NODES), jnp.float32) ** level_of(seeds[3], (SUBS, NODES), ((0, 128),), -0.2, 0.2), 0.95, 0.995)
    port_node = place_ends(jax.random.randint(seeds[4], (SUBS, 4, CAP), 0, NODES), jax.random.fold_in(seeds[4], 1), 0, NODES - 1).astype(jnp.int32)
    line_count = draw_line_count(jax.random.fold_in(seeds[14], 71), 0)
    line_delay = draw_line_delay(jax.random.fold_in(seeds[14], 71), 0)
    line_admittance = jnp.clip(jnp.exp(math.log(1.2) - 1.3862944 * jax.random.uniform(seeds[7], (SUBS, 4, CAP), jnp.float32) ** level_of(seeds[7], (SUBS, 4, CAP), ((0, 128),), -0.2, 0.2)), 0.3, 1.2)
    later_history = bell_draw(seeds[8], (SUBS, 4, CAP, 2 * BLOCK, SCEN), 1.0, 6.0, ((0, 128), (4, 4)), jnp.float32)
    conv_node = place_ends(jax.random.randint(seeds[9], (SUBS, CONV), 0, NODES), jax.random.fold_in(seeds[9], 1), 0, NODES - 1).astype(jnp.int32)
    conv_drive = bell_draw(seeds[10], (SUBS, STEPS, SCEN, CONV), (1.0 / (STEPS * SCEN) ** 0.5), 0.25, ((0, 128), (2, 4)), jnp.float32)
    fault_bus = place_ends(jax.random.randint(seeds[11], (SCEN,), 0, SUBS * NODES), jax.random.fold_in(seeds[11], 1), 0, (SUBS * NODES) - 1).astype(jnp.int32)
    fault_current = bell_draw(seeds[12], (STEPS, SCEN), 2.0, 12.0, ((1, 4),), jnp.float32)
    fault_voltage = bell_draw(seeds[13], (STEPS, SCEN), (1.0 / STEPS ** 0.5), 2.0, ((1, 4),), jnp.float32)
    return dict(inverse_matrix=inverse_matrix, objective_grad=objective_grad, final_adjoint=final_adjoint, companion=companion, port_node=port_node, line_count=line_count, line_delay=line_delay, line_admittance=line_admittance, later_history=later_history, conv_node=conv_node, conv_drive=conv_drive, fault_bus=fault_bus, fault_current=fault_current, fault_voltage=fault_voltage)


PRECISE = lax.Precision.HIGHEST


def partner_values(series):
    offsets = (1, -1, GRIDW, -GRIDW)
    opposite = (1, 0, 3, 2)
    return jnp.stack([jnp.roll(series[:, opposite[direction]], -offsets[direction], axis=0) for direction in range(4)], axis=1)


def reference(inverse_matrix, objective_grad, final_adjoint, companion, port_node, line_count, line_delay, line_admittance, later_history, conv_node, conv_drive, fault_bus, fault_current, fault_voltage):
    live_mask = (jnp.arange(CAP, dtype=jnp.int32)[None, None, :] < line_count[:, :, None]).astype(jnp.float32)
    weights = inverse_matrix.astype(jnp.float32)
    port_flat = port_node.reshape(SUBS, 4 * CAP)
    node_ids = jnp.arange(SUBS * NODES, dtype=jnp.int32).reshape(SUBS, NODES)
    fault_mask = (node_ids[:, None, :] == fault_bus[None, :, None]).astype(jnp.float32)
    line_scale = (line_admittance * live_mask).reshape(SUBS, 4 * CAP)
    drive_steps = jnp.moveaxis(conv_drive, 1, 0)
    window = later_history
    adjoint_next = final_adjoint
    control_sens = jnp.zeros((SUBS, CONV), jnp.float32)
    fault_sens = jnp.zeros((SCEN,), jnp.float32)
    block_rows = jnp.arange(BLOCK, dtype=jnp.int32)

    def one_step(adjoint_prev, inputs):
        grad_now, inflow_now, current_now, drive_now, volt_now = inputs
        line_in = jax.vmap(lambda port_list, value_block: jnp.zeros((SCEN, NODES), jnp.float32).at[:, port_list].add(value_block))(port_flat, inflow_now)
        right_side = grad_now.astype(jnp.float32) + companion[:, None, :] * adjoint_prev + line_in + current_now[None, :, None] * fault_mask
        rounded = lax.optimization_barrier(right_side.astype(jnp.bfloat16)).astype(jnp.float32)
        adjoint = jnp.einsum("psn,pnm->psm", rounded, weights, precision=PRECISE)
        at_ports = jax.vmap(lambda row_block, port_list: row_block[:, port_list])(adjoint, port_flat)
        at_conv = jax.vmap(lambda row_block, port_list: row_block[:, port_list])(adjoint, conv_node)
        control_term = jnp.sum(at_conv * drive_now, axis=1)
        fault_term = jnp.sum(adjoint * fault_mask, axis=(0, 2)) * volt_now
        return adjoint, (at_ports, control_term, fault_term)

    for block_id in reversed(range(BLOCKS)):
        block_start = block_id * BLOCK
        block_slice = slice(block_start, block_start + BLOCK)
        target = block_rows[None, None, None, :] + line_delay[:, :, :, None] - BLOCK
        target = jnp.broadcast_to(target[..., None], (SUBS, 4, CAP, BLOCK, SCEN)).astype(jnp.int32)
        picked = jnp.take_along_axis(window, target, axis=3)
        inflow = jnp.transpose(picked.reshape(SUBS, 4 * CAP, BLOCK, SCEN), (2, 0, 3, 1)) * line_scale[None, :, None, :]
        adjoint_next, (at_ports, control_terms, fault_terms) = lax.scan(one_step, adjoint_next, (objective_grad[block_slice], inflow, fault_current[block_slice], drive_steps[block_slice], fault_voltage[block_slice]), reverse=True)
        control_sens = control_sens + jnp.sum(control_terms, axis=0)
        fault_sens = fault_sens + jnp.sum(fault_terms, axis=0)
        series = jnp.transpose(at_ports.reshape(BLOCK, SUBS, SCEN, 4, CAP), (1, 3, 4, 0, 2)) * live_mask[..., None, None]
        window = jnp.concatenate([partner_values(series), window[:, :, :, :BLOCK]], axis=3)
    return adjoint_next, window, control_sens, fault_sens
```

```python
import jax
import jax.numpy as jnp
import numpy as np
from jax.sharding import Mesh
from jax import lax
from jax.sharding import PartitionSpec as P

PRECISE = lax.Precision.HIGHEST


SUB = ("z_hi", "x", "y", "core")
SUB_SIZES = (2, 4, 8, 2)


def sum_over_sub(value):
    for axis in reversed(SUB):
        value = lax.psum(value, axis)
    return value


def passed_along(value, axis, steps):
    count = lax.axis_size(axis)
    pairs = [(source, (source + steps) % count) for source in range(count)]
    return lax.ppermute(value, axis, pairs)


def body(
    inverse_matrix,
    objective_grad,
    final_adjoint,
    companion,
    port_node,
    line_count,
    line_delay,
    line_admittance,
    later_history,
    conv_node,
    conv_drive,
    fault_bus,
    fault_current,
    fault_voltage,
):
    node_count = inverse_matrix.shape[1]
    scen_rows = objective_grad.shape[2]
    slot_count = port_node.shape[2]
    port_total = 4 * slot_count
    conv_count = conv_node.shape[1]
    block_len = later_history.shape[3] // 2
    blocks = objective_grad.shape[0] // block_len
    sub_count = lax.axis_size(SUB)
    grid_width = max(2, sub_count // 16)
    offsets = (1, -1, grid_width, -grid_width)
    opposite = (1, 0, 3, 2)
    sub_index = lax.axis_index(SUB)
    weights = inverse_matrix[0]
    live_mask = (lax.iota(jnp.int32, slot_count)[None, :] < line_count[0][:, None]).astype(
        jnp.float32
    )
    node_iota = lax.iota(jnp.int32, node_count)
    pick_table = jnp.concatenate(
        [
            node_iota[:, None] == port_node[0].reshape(port_total)[None, :],
            node_iota[:, None] == conv_node[0][None, :],
        ],
        axis=1,
    ).astype(jnp.float32)
    spread_table = jnp.transpose(pick_table[:, :port_total])
    line_scale = (line_admittance[0] * live_mask).reshape(port_total)
    fault_table = (node_iota[None, :] == (fault_bus - sub_index * node_count)[:, None]).astype(
        jnp.float32
    )
    window = later_history[0]
    adjoint_next = final_adjoint[0]
    control_local = jnp.zeros((conv_count,), jnp.float32)
    fault_local = jnp.zeros((scen_rows,), jnp.float32)
    block_rows = lax.iota(jnp.int32, block_len)
    time_iota = lax.iota(jnp.int32, 2 * block_len)

    def one_step(adjoint_prev, inputs):
        grad_now, inflow_now, current_now = inputs
        right_side = (
            grad_now.astype(jnp.float32)
            + companion[0][None, :] * adjoint_prev
            + inflow_now
            + current_now[:, None] * fault_table
        )
        adjoint = jnp.dot(
            right_side.astype(jnp.bfloat16), weights, preferred_element_type=jnp.float32
        )
        return (adjoint, adjoint)

    for block_id in reversed(range(blocks)):
        block_start = block_id * block_len
        target = block_rows[None, None, :] + line_delay[0][:, :, None] - block_len
        time_table = (target[..., None] == time_iota).astype(jnp.float32)
        picked = (
            jnp.einsum("ecji,ecis->jsec", time_table, window, precision=PRECISE).reshape(
                block_len * scen_rows, port_total
            )
            * line_scale[None, :]
        )
        inflow = jnp.dot(picked, spread_table, precision=PRECISE).reshape(
            block_len, scen_rows, node_count
        )
        adjoint_next, adjoint_block = lax.scan(
            one_step,
            adjoint_next,
            (
                objective_grad[block_start : block_start + block_len, 0],
                inflow,
                fault_current[block_start : block_start + block_len],
            ),
            reverse=True,
        )
        samples = jnp.dot(
            adjoint_block.reshape(block_len * scen_rows, node_count), pick_table, precision=PRECISE
        )
        series = (
            jnp.transpose(
                samples[:, :port_total].reshape(block_len, scen_rows, 4, slot_count), (2, 3, 0, 1)
            )
            * live_mask[:, :, None, None]
        )
        outbound = series.reshape(4, slot_count, block_len * scen_rows)
        control_term = jnp.sum(
            samples[:, port_total:].reshape(block_len, scen_rows, conv_count)
            * conv_drive[0, block_start : block_start + block_len],
            axis=(0, 1),
        )
        fault_term = jnp.sum(
            jnp.sum(adjoint_block * fault_table[None], axis=2)
            * fault_voltage[block_start : block_start + block_len],
            axis=0,
        )
        control_local = control_local + lax.psum(control_term, "scen")
        fault_local = fault_local + fault_term
        received = jnp.stack(
            [
                passed_along(outbound[opposite[direction]], SUB, -offsets[direction])
                for direction in range(4)
            ]
        )
        window = jnp.concatenate(
            [received.reshape(4, slot_count, block_len, scen_rows), window[:, :, :block_len]],
            axis=2,
        )
    fault_local = sum_over_sub(fault_local)
    return (adjoint_next[None], window[None], control_local[None], fault_local)


def solution(mesh):
    sub_mesh = Mesh(
        np.asarray(mesh.devices).reshape(SUB_SIZES + (mesh.shape["scen"],)), SUB + ("scen",)
    )
    return jax.shard_map(
        body,
        mesh=sub_mesh,
        in_specs=(
            P(SUB, None, None),
            P(None, SUB, "scen", None),
            P(SUB, "scen", None),
            P(SUB, None),
            P(SUB, None, None),
            P(SUB, None),
            P(SUB, None, None),
            P(SUB, None, None),
            P(SUB, None, None, None, "scen"),
            P(SUB, None),
            P(SUB, None, "scen", None),
            P("scen"),
            P(None, "scen"),
            P(None, "scen"),
        ),
        out_specs=(
            P(SUB, "scen", None),
            P(SUB, None, None, None, "scen"),
            P(SUB, None),
            P("scen"),
        ),
        check_vma=False,
    )
```

```python
import jax
import jax.numpy as jnp
import numpy as np
from jax.sharding import Mesh
from jax.experimental import pallas as pl
from jax import lax
from jax.sharding import PartitionSpec as P

PRECISE = lax.Precision.HIGHEST


SUB = ("z_hi", "x", "y", "core")
SUB_SIZES = (2, 4, 8, 2)


def sum_over_sub(value):
    for axis in reversed(SUB):
        value = lax.psum(value, axis)
    return value


def block_scan_kernel(
    grad_ref, inflow_ref, current_ref, fault_ref, companion_ref, start_ref, weights_ref, out_ref, last_ref
):
    steps = grad_ref.shape[0]
    companion = companion_ref[...]
    fault_table = fault_ref[...]

    def one_step(index, adjoint_prev):
        step = steps - 1 - index
        right_side = (
            grad_ref[step].astype(jnp.float32)
            + companion * adjoint_prev
            + inflow_ref[step]
            + current_ref[step] * fault_table
        )
        adjoint = jnp.dot(
            right_side.astype(jnp.bfloat16), weights_ref[...], preferred_element_type=jnp.float32
        )
        out_ref[step] = adjoint
        return adjoint

    last_ref[...] = lax.fori_loop(0, steps, one_step, start_ref[...])


def block_scan(grad, inflow, current, fault_table, companion, start, weights):
    return pl.pallas_call(
        block_scan_kernel,
        out_shape=(
            jax.ShapeDtypeStruct(inflow.shape, jnp.float32),
            jax.ShapeDtypeStruct(start.shape, jnp.float32),
        ),
    )(grad, inflow, current[:, :, None], fault_table, companion, start, weights)


def passed_along(value, axis, steps):
    count = lax.axis_size(axis)
    pairs = [(source, (source + steps) % count) for source in range(count)]
    return lax.ppermute(value, axis, pairs)


def body(
    inverse_matrix,
    objective_grad,
    final_adjoint,
    companion,
    port_node,
    line_count,
    line_delay,
    line_admittance,
    later_history,
    conv_node,
    conv_drive,
    fault_bus,
    fault_current,
    fault_voltage,
):
    node_count = inverse_matrix.shape[1]
    scen_rows = objective_grad.shape[2]
    slot_count = port_node.shape[2]
    port_total = 4 * slot_count
    conv_count = conv_node.shape[1]
    block_len = later_history.shape[3] // 2
    blocks = objective_grad.shape[0] // block_len
    sub_count = lax.axis_size(SUB)
    grid_width = max(2, sub_count // 16)
    offsets = (1, -1, grid_width, -grid_width)
    opposite = (1, 0, 3, 2)
    sub_index = lax.axis_index(SUB)
    weights = inverse_matrix[0]
    live_mask = (lax.iota(jnp.int32, slot_count)[None, :] < line_count[0][:, None]).astype(
        jnp.float32
    )
    node_iota = lax.iota(jnp.int32, node_count)
    pick_table = jnp.concatenate(
        [
            node_iota[:, None] == port_node[0].reshape(port_total)[None, :],
            node_iota[:, None] == conv_node[0][None, :],
        ],
        axis=1,
    ).astype(jnp.float32)
    spread_table = jnp.transpose(pick_table[:, :port_total])
    line_scale = (line_admittance[0] * live_mask).reshape(port_total)
    fault_table = (node_iota[None, :] == (fault_bus - sub_index * node_count)[:, None]).astype(
        jnp.float32
    )
    window = later_history[0]
    adjoint_next = final_adjoint[0]
    control_local = jnp.zeros((conv_count,), jnp.float32)
    fault_local = jnp.zeros((scen_rows,), jnp.float32)
    block_rows = lax.iota(jnp.int32, block_len)
    time_iota = lax.iota(jnp.int32, 2 * block_len)


    for block_id in reversed(range(blocks)):
        block_start = block_id * block_len
        target = block_rows[None, None, :] + line_delay[0][:, :, None] - block_len
        time_table = (target[..., None] == time_iota).astype(jnp.float32)
        picked = (
            jnp.einsum("ecji,ecis->jsec", time_table, window, precision=PRECISE).reshape(
                block_len * scen_rows, port_total
            )
            * line_scale[None, :]
        )
        inflow = jnp.dot(picked, spread_table, precision=PRECISE).reshape(
            block_len, scen_rows, node_count
        )
        adjoint_block, adjoint_next = block_scan(
            objective_grad[block_start : block_start + block_len, 0],
            inflow,
            fault_current[block_start : block_start + block_len],
            fault_table,
            companion,
            adjoint_next,
            weights,
        )
        samples = jnp.dot(
            adjoint_block.reshape(block_len * scen_rows, node_count), pick_table, precision=PRECISE
        )
        series = (
            jnp.transpose(
                samples[:, :port_total].reshape(block_len, scen_rows, 4, slot_count), (2, 3, 0, 1)
            )
            * live_mask[:, :, None, None]
        )
        outbound = series.reshape(4, slot_count, block_len * scen_rows)
        control_term = jnp.sum(
            samples[:, port_total:].reshape(block_len, scen_rows, conv_count)
            * conv_drive[0, block_start : block_start + block_len],
            axis=(0, 1),
        )
        fault_term = jnp.sum(
            jnp.sum(adjoint_block * fault_table[None], axis=2)
            * fault_voltage[block_start : block_start + block_len],
            axis=0,
        )
        control_local = control_local + lax.psum(control_term, "scen")
        fault_local = fault_local + fault_term
        received = jnp.stack(
            [
                passed_along(outbound[opposite[direction]], SUB, -offsets[direction])
                for direction in range(4)
            ]
        )
        window = jnp.concatenate(
            [received.reshape(4, slot_count, block_len, scen_rows), window[:, :, :block_len]],
            axis=2,
        )
    fault_local = sum_over_sub(fault_local)
    return (adjoint_next[None], window[None], control_local[None], fault_local)


def solution(mesh):
    sub_mesh = Mesh(
        np.asarray(mesh.devices).reshape(SUB_SIZES + (mesh.shape["scen"],)), SUB + ("scen",)
    )
    return jax.shard_map(
        body,
        mesh=sub_mesh,
        in_specs=(
            P(SUB, None, None),
            P(None, SUB, "scen", None),
            P(SUB, "scen", None),
            P(SUB, None),
            P(SUB, None, None),
            P(SUB, None),
            P(SUB, None, None),
            P(SUB, None, None),
            P(SUB, None, None, None, "scen"),
            P(SUB, None),
            P(SUB, None, "scen", None),
            P("scen"),
            P(None, "scen"),
            P(None, "scen"),
        ),
        out_specs=(
            P(SUB, "scen", None),
            P(SUB, None, None, None, "scen"),
            P(SUB, None),
            P("scen"),
        ),
        check_vma=False,
    )
```

```python
import jax
import jax.numpy as jnp
import numpy as np
from jax.sharding import Mesh
from jax.experimental import pallas as pl
from jax import lax
from jax.sharding import PartitionSpec as P

PRECISE = lax.Precision.HIGHEST


SUB = ("z_hi", "x", "y", "core")
SUB_SIZES = (2, 4, 8, 2)


def sum_both(fault_value, control_value):
    for axis in reversed(SUB[1:]):
        fault_value = lax.psum(fault_value, axis)
    scen_index = lax.axis_index("scen")
    high_index = lax.axis_index(SUB[0])
    fault_slots = jnp.zeros((lax.axis_size("scen"),) + fault_value.shape, jnp.float32)
    control_slots = jnp.zeros((lax.axis_size(SUB[0]),) + control_value.shape, jnp.float32)
    fault_slots, control_slots = lax.psum(
        (fault_slots.at[scen_index].set(fault_value), control_slots.at[high_index].set(control_value)),
        (SUB[0], "scen"),
    )
    return fault_slots[scen_index], control_slots[high_index]


def block_scan_kernel(
    grad_ref, inflow_ref, current_ref, fault_ref, companion_ref, start_ref, weights_ref, out_ref, last_ref
):
    steps = grad_ref.shape[0]
    companion = companion_ref[...]
    fault_table = fault_ref[...]

    def one_step(index, adjoint_prev):
        step = steps - 1 - index
        right_side = (
            grad_ref[step].astype(jnp.float32)
            + companion * adjoint_prev
            + inflow_ref[step]
            + current_ref[step] * fault_table
        )
        adjoint = jnp.dot(
            right_side.astype(jnp.bfloat16), weights_ref[...], preferred_element_type=jnp.float32
        )
        out_ref[step] = adjoint
        return adjoint

    last_ref[...] = lax.fori_loop(0, steps, one_step, start_ref[...])


def block_scan(grad, inflow, current, fault_table, companion, start, weights):
    return pl.pallas_call(
        block_scan_kernel,
        out_shape=(
            jax.ShapeDtypeStruct(inflow.shape, jnp.float32),
            jax.ShapeDtypeStruct(start.shape, jnp.float32),
        ),
    )(grad, inflow, current[:, :, None], fault_table, companion, start, weights)


def passed_along(value, axis, steps):
    count = lax.axis_size(axis)
    pairs = [(source, (source + steps) % count) for source in range(count)]
    return lax.ppermute(value, axis, pairs)


def body(
    inverse_matrix,
    objective_grad,
    final_adjoint,
    companion,
    port_node,
    line_count,
    line_delay,
    line_admittance,
    later_history,
    conv_node,
    conv_drive,
    fault_bus,
    fault_current,
    fault_voltage,
):
    node_count = inverse_matrix.shape[1]
    scen_rows = objective_grad.shape[2]
    slot_count = port_node.shape[2]
    port_total = 4 * slot_count
    conv_count = conv_node.shape[1]
    block_len = later_history.shape[3] // 2
    blocks = objective_grad.shape[0] // block_len
    sub_count = lax.axis_size(SUB)
    grid_width = max(2, sub_count // 16)
    offsets = (1, -1, grid_width, -grid_width)
    opposite = (1, 0, 3, 2)
    sub_index = lax.axis_index(SUB)
    weights = inverse_matrix[0]
    live_mask = (lax.iota(jnp.int32, slot_count)[None, :] < line_count[0][:, None]).astype(
        jnp.float32
    )
    node_iota = lax.iota(jnp.int32, node_count)
    pick_table = jnp.concatenate(
        [
            node_iota[:, None] == port_node[0].reshape(port_total)[None, :],
            node_iota[:, None] == conv_node[0][None, :],
        ],
        axis=1,
    ).astype(jnp.float32)
    spread_table = jnp.transpose(pick_table[:, :port_total])
    line_scale = (line_admittance[0] * live_mask).reshape(port_total)
    fault_table = (node_iota[None, :] == (fault_bus - sub_index * node_count)[:, None]).astype(
        jnp.float32
    )
    window = later_history[0]
    adjoint_next = final_adjoint[0]
    control_local = jnp.zeros((conv_count,), jnp.float32)
    fault_local = jnp.zeros((scen_rows,), jnp.float32)
    block_rows = lax.iota(jnp.int32, block_len)
    time_iota = lax.iota(jnp.int32, 2 * block_len)


    for block_id in reversed(range(blocks)):
        block_start = block_id * block_len
        target = block_rows[None, None, :] + line_delay[0][:, :, None] - block_len
        time_table = (target[..., None] == time_iota).astype(jnp.float32)
        picked = (
            jnp.einsum("ecji,ecis->jsec", time_table, window, precision=PRECISE).reshape(
                block_len * scen_rows, port_total
            )
            * line_scale[None, :]
        )
        inflow = jnp.dot(picked, spread_table, precision=PRECISE).reshape(
            block_len, scen_rows, node_count
        )
        adjoint_block, adjoint_next = block_scan(
            objective_grad[block_start : block_start + block_len, 0],
            inflow,
            fault_current[block_start : block_start + block_len],
            fault_table,
            companion,
            adjoint_next,
            weights,
        )
        samples = jnp.dot(
            adjoint_block.reshape(block_len * scen_rows, node_count), pick_table, precision=PRECISE
        )
        series = (
            jnp.transpose(
                samples[:, :port_total].reshape(block_len, scen_rows, 4, slot_count), (2, 3, 0, 1)
            )
            * live_mask[:, :, None, None]
        )
        outbound = series.reshape(4, slot_count, block_len * scen_rows)
        control_term = jnp.sum(
            samples[:, port_total:].reshape(block_len, scen_rows, conv_count)
            * conv_drive[0, block_start : block_start + block_len],
            axis=(0, 1),
        )
        fault_term = jnp.sum(
            jnp.sum(adjoint_block * fault_table[None], axis=2)
            * fault_voltage[block_start : block_start + block_len],
            axis=0,
        )
        control_local = control_local + control_term
        fault_local = fault_local + fault_term
        received = jnp.stack(
            [
                passed_along(outbound[opposite[direction]], SUB, -offsets[direction])
                for direction in range(4)
            ]
        )
        window = jnp.concatenate(
            [received.reshape(4, slot_count, block_len, scen_rows), window[:, :, :block_len]],
            axis=2,
        )
    fault_local, control_local = sum_both(fault_local, control_local)
    return (adjoint_next[None], window[None], control_local[None], fault_local)


def solution(mesh):
    sub_mesh = Mesh(
        np.asarray(mesh.devices).reshape(SUB_SIZES + (mesh.shape["scen"],)), SUB + ("scen",)
    )
    return jax.shard_map(
        body,
        mesh=sub_mesh,
        in_specs=(
            P(SUB, None, None),
            P(None, SUB, "scen", None),
            P(SUB, "scen", None),
            P(SUB, None),
            P(SUB, None, None),
            P(SUB, None),
            P(SUB, None, None),
            P(SUB, None, None),
            P(SUB, None, None, None, "scen"),
            P(SUB, None),
            P(SUB, None, "scen", None),
            P("scen"),
            P(None, "scen"),
            P(None, "scen"),
        ),
        out_specs=(
            P(SUB, "scen", None),
            P(SUB, None, None, None, "scen"),
            P(SUB, None),
            P("scen"),
        ),
        check_vma=False,
    )
```

```python
import jax
import jax.numpy as jnp
import numpy as np
from jax.sharding import Mesh
from jax.experimental import pallas as pl
from jax import lax
from jax.sharding import PartitionSpec as P

PRECISE = lax.Precision.HIGHEST


SUB = ("z_hi", "x", "y", "core")
SUB_SIZES = (2, 4, 8, 2)


def sum_both(fault_value, control_value):
    for axis in reversed(SUB[1:]):
        fault_value = lax.psum(fault_value, axis)
    scen_index = lax.axis_index("scen")
    high_index = lax.axis_index(SUB[0])
    fault_slots = jnp.zeros((lax.axis_size("scen"),) + fault_value.shape, jnp.float32)
    control_slots = jnp.zeros((lax.axis_size(SUB[0]),) + control_value.shape, jnp.float32)
    fault_slots, control_slots = lax.psum(
        (fault_slots.at[scen_index].set(fault_value), control_slots.at[high_index].set(control_value)),
        (SUB[0], "scen"),
    )
    return fault_slots[scen_index], control_slots[high_index]


def block_scan_kernel(
    grad_ref, inflow_ref, current_ref, fault_ref, companion_ref, start_ref, weights_ref, out_ref, last_ref
):
    steps = grad_ref.shape[0]
    companion = companion_ref[...]
    fault_table = fault_ref[...]

    def one_step(index, adjoint_prev):
        step = steps - 1 - index
        right_side = (
            grad_ref[step].astype(jnp.float32)
            + companion * adjoint_prev
            + inflow_ref[step]
            + current_ref[step] * fault_table
        )
        adjoint = jnp.dot(
            right_side.astype(jnp.bfloat16), weights_ref[...], preferred_element_type=jnp.float32
        )
        out_ref[step] = adjoint
        return adjoint

    last_ref[...] = lax.fori_loop(0, steps, one_step, start_ref[...])


def block_scan(grad, inflow, current, fault_table, companion, start, weights):
    return pl.pallas_call(
        block_scan_kernel,
        out_shape=(
            jax.ShapeDtypeStruct(inflow.shape, jnp.float32),
            jax.ShapeDtypeStruct(start.shape, jnp.float32),
        ),
    )(grad, inflow, current[:, :, None], fault_table, companion, start, weights)


def passed_along(value, axis, steps):
    count = lax.axis_size(axis)
    pairs = [(source, (source + steps) % count) for source in range(count)]
    return lax.ppermute(value, axis, pairs)


def body(
    inverse_matrix,
    objective_grad,
    final_adjoint,
    companion,
    port_node,
    line_count,
    line_delay,
    line_admittance,
    later_history,
    conv_node,
    conv_drive,
    fault_bus,
    fault_current,
    fault_voltage,
):
    node_count = inverse_matrix.shape[1]
    scen_rows = objective_grad.shape[2]
    slot_count = port_node.shape[2]
    port_total = 4 * slot_count
    conv_count = conv_node.shape[1]
    block_len = later_history.shape[3] // 2
    blocks = objective_grad.shape[0] // block_len
    sub_count = lax.axis_size(SUB)
    grid_width = max(2, sub_count // 16)
    offsets = (1, -1, grid_width, -grid_width)
    opposite = (1, 0, 3, 2)
    sub_index = lax.axis_index(SUB)
    weights = inverse_matrix[0]
    live_mask = (lax.iota(jnp.int32, slot_count)[None, :] < line_count[0][:, None]).astype(
        jnp.float32
    )
    node_iota = lax.iota(jnp.int32, node_count)
    pick_table = jnp.concatenate(
        [
            node_iota[:, None] == port_node[0].reshape(port_total)[None, :],
            node_iota[:, None] == conv_node[0][None, :],
        ],
        axis=1,
    ).astype(jnp.float32)
    spread_table = jnp.transpose(pick_table[:, :port_total])
    line_scale = (line_admittance[0] * live_mask).reshape(port_total)
    fault_table = (node_iota[None, :] == (fault_bus - sub_index * node_count)[:, None]).astype(
        jnp.float32
    )
    window = later_history[0]
    adjoint_next = final_adjoint[0]
    control_local = jnp.zeros((conv_count,), jnp.float32)
    fault_local = jnp.zeros((scen_rows,), jnp.float32)
    block_rows = lax.iota(jnp.int32, block_len)
    time_iota = lax.iota(jnp.int32, 2 * block_len)


    for block_id in reversed(range(blocks)):
        block_start = block_id * block_len
        target = block_rows[None, None, :] + line_delay[0][:, :, None] - block_len
        time_table = (target[..., None] == time_iota).astype(jnp.float32)
        picked = (
            jnp.einsum("ecji,ecis->jsec", time_table, window, precision=PRECISE).reshape(
                block_len * scen_rows, port_total
            )
            * line_scale[None, :]
        )
        inflow = jnp.dot(picked, spread_table, precision=PRECISE).reshape(
            block_len, scen_rows, node_count
        )
        adjoint_block, adjoint_next = block_scan(
            objective_grad[block_start : block_start + block_len, 0],
            inflow,
            fault_current[block_start : block_start + block_len],
            fault_table,
            companion,
            adjoint_next,
            weights,
        )
        samples = jnp.dot(
            adjoint_block.reshape(block_len * scen_rows, node_count), pick_table, precision=PRECISE
        )
        fault_term = jnp.sum(
            jnp.sum(adjoint_block * fault_table[None], axis=2)
            * fault_voltage[block_start : block_start + block_len],
            axis=0,
        )
        samples, fault_term = lax.optimization_barrier((samples, fault_term))
        series = (
            jnp.transpose(
                samples[:, :port_total].reshape(block_len, scen_rows, 4, slot_count), (2, 3, 0, 1)
            )
            * live_mask[:, :, None, None]
        )
        outbound = series.reshape(4, slot_count, block_len * scen_rows)
        control_term = jnp.sum(
            samples[:, port_total:].reshape(block_len, scen_rows, conv_count)
            * conv_drive[0, block_start : block_start + block_len],
            axis=(0, 1),
        )
        control_local = control_local + control_term
        fault_local = fault_local + fault_term
        received = jnp.stack(
            [
                passed_along(outbound[opposite[direction]], SUB, -offsets[direction])
                for direction in range(4)
            ]
        )
        window = jnp.concatenate(
            [received.reshape(4, slot_count, block_len, scen_rows), window[:, :, :block_len]],
            axis=2,
        )
    fault_local, control_local = sum_both(fault_local, control_local)
    return (adjoint_next[None], window[None], control_local[None], fault_local)


def solution(mesh):
    sub_mesh = Mesh(
        np.asarray(mesh.devices).reshape(SUB_SIZES + (mesh.shape["scen"],)), SUB + ("scen",)
    )
    return jax.shard_map(
        body,
        mesh=sub_mesh,
        in_specs=(
            P(SUB, None, None),
            P(None, SUB, "scen", None),
            P(SUB, "scen", None),
            P(SUB, None),
            P(SUB, None, None),
            P(SUB, None),
            P(SUB, None, None),
            P(SUB, None, None),
            P(SUB, None, None, None, "scen"),
            P(SUB, None),
            P(SUB, None, "scen", None),
            P("scen"),
            P(None, "scen"),
            P(None, "scen"),
        ),
        out_specs=(
            P(SUB, "scen", None),
            P(SUB, None, None, None, "scen"),
            P(SUB, None),
            P("scen"),
        ),
        check_vma=False,
    )
```

```python
import jax
import jax.numpy as jnp
import numpy as np
from jax.sharding import Mesh
from jax.experimental import pallas as pl
from jax.experimental.pallas import tpu as pltpu
from jax import lax
from jax.sharding import PartitionSpec as P

PRECISE = lax.Precision.HIGHEST


SUB = ("z_hi", "x", "y", "core")
SUB_SIZES = (2, 4, 8, 2)


def sum_both(fault_value, control_value):
    for axis in reversed(SUB[1:]):
        fault_value = lax.psum(fault_value, axis)
    scen_index = lax.axis_index("scen")
    high_index = lax.axis_index(SUB[0])
    fault_slots = jnp.zeros((lax.axis_size("scen"),) + fault_value.shape, jnp.float32)
    control_slots = jnp.zeros((lax.axis_size(SUB[0]),) + control_value.shape, jnp.float32)
    fault_slots, control_slots = lax.psum(
        (fault_slots.at[scen_index].set(fault_value), control_slots.at[high_index].set(control_value)),
        (SUB[0], "scen"),
    )
    return fault_slots[scen_index], control_slots[high_index]


def block_scan_kernel(
    grad_ref,
    picked_ref,
    spread_ref,
    current_ref,
    fault_ref,
    companion_ref,
    start_ref,
    weights_ref,
    pick_ref,
    voltage_ref,
    last_ref,
    samples_ref,
    fault_out_ref,
    inflow_ref,
    adjoint_ref,
):
    steps, scen_rows, node_count = grad_ref.shape
    companion = companion_ref[...]
    fault_table = fault_ref[...]
    inflow_ref[...] = jnp.dot(
        picked_ref[...], spread_ref[...], precision=PRECISE, preferred_element_type=jnp.float32
    )

    def one_step(index, adjoint_prev):
        step = steps - 1 - index
        rows = pl.ds(pl.multiple_of(step * scen_rows, scen_rows), scen_rows)
        right_side = (
            grad_ref[step].astype(jnp.float32)
            + companion * adjoint_prev
            + inflow_ref[rows]
            + current_ref[step] * fault_table
        )
        adjoint = jnp.dot(
            right_side.astype(jnp.bfloat16), weights_ref[...], preferred_element_type=jnp.float32
        )
        adjoint_ref[rows] = adjoint
        return adjoint

    last_ref[...] = lax.fori_loop(0, steps, one_step, start_ref[...])
    adjoint_block = adjoint_ref[...]
    samples_ref[...] = jnp.dot(
        adjoint_block, pick_ref[...], precision=PRECISE, preferred_element_type=jnp.float32
    )
    at_fault = jnp.sum(adjoint_block.reshape(steps, scen_rows, node_count) * fault_table[None], axis=2)
    fault_out_ref[...] = jnp.sum(at_fault * voltage_ref[...], axis=0, keepdims=True)


def block_scan(grad, picked, spread, current, fault_table, companion, start, weights, pick, voltage):
    steps, scen_rows, node_count = grad.shape
    return pl.pallas_call(
        block_scan_kernel,
        out_shape=(
            jax.ShapeDtypeStruct(start.shape, jnp.float32),
            jax.ShapeDtypeStruct((steps * scen_rows, pick.shape[1]), jnp.float32),
            jax.ShapeDtypeStruct((1, scen_rows), jnp.float32),
        ),
        scratch_shapes=[
            pltpu.VMEM((steps * scen_rows, node_count), jnp.float32),
            pltpu.VMEM((steps * scen_rows, node_count), jnp.float32),
        ],
    )(grad, picked, spread, current[:, :, None], fault_table, companion, start, weights, pick, voltage)


def passed_along(value, axis, steps):
    count = lax.axis_size(axis)
    pairs = [(source, (source + steps) % count) for source in range(count)]
    return lax.ppermute(value, axis, pairs)


def body(
    inverse_matrix,
    objective_grad,
    final_adjoint,
    companion,
    port_node,
    line_count,
    line_delay,
    line_admittance,
    later_history,
    conv_node,
    conv_drive,
    fault_bus,
    fault_current,
    fault_voltage,
):
    node_count = inverse_matrix.shape[1]
    scen_rows = objective_grad.shape[2]
    slot_count = port_node.shape[2]
    port_total = 4 * slot_count
    conv_count = conv_node.shape[1]
    block_len = later_history.shape[3] // 2
    blocks = objective_grad.shape[0] // block_len
    sub_count = lax.axis_size(SUB)
    grid_width = max(2, sub_count // 16)
    offsets = (1, -1, grid_width, -grid_width)
    opposite = (1, 0, 3, 2)
    sub_index = lax.axis_index(SUB)
    weights = inverse_matrix[0]
    live_mask = (lax.iota(jnp.int32, slot_count)[None, :] < line_count[0][:, None]).astype(
        jnp.float32
    )
    node_iota = lax.iota(jnp.int32, node_count)
    pick_table = jnp.concatenate(
        [
            node_iota[:, None] == port_node[0].reshape(port_total)[None, :],
            node_iota[:, None] == conv_node[0][None, :],
        ],
        axis=1,
    ).astype(jnp.float32)
    spread_table = jnp.transpose(pick_table[:, :port_total])
    line_scale = (line_admittance[0] * live_mask).reshape(port_total)
    fault_table = (node_iota[None, :] == (fault_bus - sub_index * node_count)[:, None]).astype(
        jnp.float32
    )
    window = later_history[0]
    adjoint_next = final_adjoint[0]
    control_local = jnp.zeros((conv_count,), jnp.float32)
    fault_local = jnp.zeros((scen_rows,), jnp.float32)
    block_rows = lax.iota(jnp.int32, block_len)
    time_iota = lax.iota(jnp.int32, 2 * block_len)


    for block_id in reversed(range(blocks)):
        block_start = block_id * block_len
        target = block_rows[None, None, :] + line_delay[0][:, :, None] - block_len
        time_table = (target[..., None] == time_iota).astype(jnp.float32)
        picked = (
            jnp.einsum("ecji,ecis->jsec", time_table, window, precision=PRECISE).reshape(
                block_len * scen_rows, port_total
            )
            * line_scale[None, :]
        )
        adjoint_next, samples, fault_term = block_scan(
            objective_grad[block_start : block_start + block_len, 0],
            picked,
            spread_table,
            fault_current[block_start : block_start + block_len],
            fault_table,
            companion,
            adjoint_next,
            weights,
            pick_table,
            fault_voltage[block_start : block_start + block_len],
        )
        samples, fault_term = lax.optimization_barrier((samples, fault_term[0]))
        series = (
            jnp.transpose(
                samples[:, :port_total].reshape(block_len, scen_rows, 4, slot_count), (2, 3, 0, 1)
            )
            * live_mask[:, :, None, None]
        )
        outbound = series.reshape(4, slot_count, block_len * scen_rows)
        control_term = jnp.sum(
            samples[:, port_total:].reshape(block_len, scen_rows, conv_count)
            * conv_drive[0, block_start : block_start + block_len],
            axis=(0, 1),
        )
        control_local = control_local + control_term
        fault_local = fault_local + fault_term
        received = jnp.stack(
            [
                passed_along(outbound[opposite[direction]], SUB, -offsets[direction])
                for direction in range(4)
            ]
        )
        window = jnp.concatenate(
            [received.reshape(4, slot_count, block_len, scen_rows), window[:, :, :block_len]],
            axis=2,
        )
    fault_local, control_local = sum_both(fault_local, control_local)
    return (adjoint_next[None], window[None], control_local[None], fault_local)


def solution(mesh):
    sub_mesh = Mesh(
        np.asarray(mesh.devices).reshape(SUB_SIZES + (mesh.shape["scen"],)), SUB + ("scen",)
    )
    return jax.shard_map(
        body,
        mesh=sub_mesh,
        in_specs=(
            P(SUB, None, None),
            P(None, SUB, "scen", None),
            P(SUB, "scen", None),
            P(SUB, None),
            P(SUB, None, None),
            P(SUB, None),
            P(SUB, None, None),
            P(SUB, None, None),
            P(SUB, None, None, None, "scen"),
            P(SUB, None),
            P(SUB, None, "scen", None),
            P("scen"),
            P(None, "scen"),
            P(None, "scen"),
        ),
        out_specs=(
            P(SUB, "scen", None),
            P(SUB, None, None, None, "scen"),
            P(SUB, None),
            P("scen"),
        ),
        check_vma=False,
    )
```

```python
import functools

import jax
import jax.numpy as jnp
import numpy as np
from jax.sharding import Mesh
from jax.experimental import pallas as pl
from jax.experimental.pallas import tpu as pltpu
from jax import lax
from jax.sharding import PartitionSpec as P

PRECISE = lax.Precision.HIGHEST


SUB = ("z_hi", "x", "y", "core")
SUB_SIZES = (2, 4, 8, 2)


def sum_both(fault_value, control_value):
    for axis in reversed(SUB[1:]):
        fault_value = lax.psum(fault_value, axis)
    scen_index = lax.axis_index("scen")
    high_index = lax.axis_index(SUB[0])
    fault_slots = jnp.zeros((lax.axis_size("scen"),) + fault_value.shape, jnp.float32)
    control_slots = jnp.zeros((lax.axis_size(SUB[0]),) + control_value.shape, jnp.float32)
    fault_slots, control_slots = lax.psum(
        (fault_slots.at[scen_index].set(fault_value), control_slots.at[high_index].set(control_value)),
        (SUB[0], "scen"),
    )
    return fault_slots[scen_index], control_slots[high_index]


def block_scan_kernel(
    block_start,
    grad_ref,
    picked_ref,
    spread_ref,
    companion_ref,
    start_ref,
    weights_ref,
    pick_ref,
    voltage_ref,
    last_ref,
    samples_ref,
    fault_out_ref,
    inflow_ref,
    adjoint_ref,
):
    steps, scen_rows, node_count = grad_ref.shape
    companion = companion_ref[...]
    inflow_ref[...] = jnp.dot(
        picked_ref[...], spread_ref[...], precision=PRECISE, preferred_element_type=jnp.float32
    )

    def one_step(index, adjoint_prev):
        step = steps - 1 - index
        rows = pl.ds(pl.multiple_of(step * scen_rows, scen_rows), scen_rows)
        right_side = (
            grad_ref[step].astype(jnp.float32)
            + companion * adjoint_prev
            + inflow_ref[rows]
        )
        adjoint = jnp.dot(
            right_side.astype(jnp.bfloat16), weights_ref[...], preferred_element_type=jnp.float32
        )
        adjoint_ref[rows] = adjoint
        return adjoint

    last_ref[...] = lax.fori_loop(0, steps, one_step, start_ref[...])
    adjoint_block = adjoint_ref[...]
    samples_ref[...] = jnp.dot(
        adjoint_block, pick_ref[...], precision=PRECISE, preferred_element_type=jnp.float32
    )
    fault_table = spread_ref[pl.ds(spread_ref.shape[0] - scen_rows, scen_rows), :]
    at_fault = jnp.sum(adjoint_block.reshape(steps, scen_rows, node_count) * fault_table[None], axis=2)
    voltage = voltage_ref[pl.ds(block_start, steps), :]
    fault_out_ref[...] = jnp.sum(at_fault * voltage, axis=0, keepdims=True)


def block_scan(block_start, grad, picked, spread, companion, start, weights, pick, voltage):
    steps, scen_rows, node_count = grad.shape
    return pl.pallas_call(
        functools.partial(block_scan_kernel, block_start),
        out_shape=(
            jax.ShapeDtypeStruct(start.shape, jnp.float32),
            jax.ShapeDtypeStruct((steps * scen_rows, pick.shape[1]), jnp.float32),
            jax.ShapeDtypeStruct((1, scen_rows), jnp.float32),
        ),
        scratch_shapes=[
            pltpu.VMEM((steps * scen_rows, node_count), jnp.float32),
            pltpu.VMEM((steps * scen_rows, node_count), jnp.float32),
        ],
    )(grad, picked, spread, companion, start, weights, pick, voltage)


def passed_along(value, axis, steps):
    count = lax.axis_size(axis)
    pairs = [(source, (source + steps) % count) for source in range(count)]
    return lax.ppermute(value, axis, pairs)


def body(
    inverse_matrix,
    objective_grad,
    final_adjoint,
    companion,
    port_node,
    line_count,
    line_delay,
    line_admittance,
    later_history,
    conv_node,
    conv_drive,
    fault_bus,
    fault_current,
    fault_voltage,
):
    node_count = inverse_matrix.shape[1]
    scen_rows = objective_grad.shape[2]
    slot_count = port_node.shape[2]
    port_total = 4 * slot_count
    conv_count = conv_node.shape[1]
    block_len = later_history.shape[3] // 2
    blocks = objective_grad.shape[0] // block_len
    sub_count = lax.axis_size(SUB)
    grid_width = max(2, sub_count // 16)
    offsets = (1, -1, grid_width, -grid_width)
    opposite = (1, 0, 3, 2)
    sub_index = lax.axis_index(SUB)
    weights = inverse_matrix[0]
    live_mask = (lax.iota(jnp.int32, slot_count)[None, :] < line_count[0][:, None]).astype(
        jnp.float32
    )
    node_iota = lax.iota(jnp.int32, node_count)
    pick_table = jnp.concatenate(
        [
            node_iota[:, None] == port_node[0].reshape(port_total)[None, :],
            node_iota[:, None] == conv_node[0][None, :],
        ],
        axis=1,
    ).astype(jnp.float32)
    line_scale = (line_admittance[0] * live_mask).reshape(port_total)
    fault_table = (node_iota[None, :] == (fault_bus - sub_index * node_count)[:, None]).astype(
        jnp.float32
    )
    spread_table = jnp.concatenate(
        [
            (port_node[0].reshape(port_total)[:, None] == node_iota[None, :]).astype(jnp.float32),
            fault_table,
        ],
        axis=0,
    )
    scen_eye = (lax.iota(jnp.int32, scen_rows)[:, None] == lax.iota(jnp.int32, scen_rows)[None, :]).astype(
        jnp.float32
    )
    window = later_history[0]
    adjoint_next = final_adjoint[0]
    control_local = jnp.zeros((conv_count,), jnp.float32)
    fault_local = jnp.zeros((scen_rows,), jnp.float32)
    block_rows = lax.iota(jnp.int32, block_len)
    time_iota = lax.iota(jnp.int32, 2 * block_len)


    for block_id in reversed(range(blocks)):
        block_start = block_id * block_len
        target = block_rows[None, None, :] + line_delay[0][:, :, None] - block_len
        time_table = (target[..., None] == time_iota).astype(jnp.float32)
        picked = jnp.concatenate(
            [
                jnp.einsum("ecji,ecis->jsec", time_table, window, precision=PRECISE).reshape(
                    block_len * scen_rows, port_total
                )
                * line_scale[None, :],
                (fault_current[block_start : block_start + block_len, :, None] * scen_eye[None]).reshape(
                    block_len * scen_rows, scen_rows
                ),
            ],
            axis=1,
        )
        adjoint_next, samples, fault_term = block_scan(
            block_start,
            objective_grad[block_start : block_start + block_len, 0],
            picked,
            spread_table,
            companion,
            adjoint_next,
            weights,
            pick_table,
            fault_voltage,
        )
        samples, fault_term = lax.optimization_barrier((samples, fault_term[0]))
        series = (
            jnp.transpose(
                samples[:, :port_total].reshape(block_len, scen_rows, 4, slot_count), (2, 3, 0, 1)
            )
            * live_mask[:, :, None, None]
        )
        outbound = series.reshape(4, slot_count, block_len * scen_rows)
        control_term = jnp.sum(
            samples[:, port_total:].reshape(block_len, scen_rows, conv_count)
            * conv_drive[0, block_start : block_start + block_len],
            axis=(0, 1),
        )
        control_local = control_local + control_term
        fault_local = fault_local + fault_term
        received = jnp.stack(
            [
                passed_along(outbound[opposite[direction]], SUB, -offsets[direction])
                for direction in range(4)
            ]
        )
        window = jnp.concatenate(
            [received.reshape(4, slot_count, block_len, scen_rows), window[:, :, :block_len]],
            axis=2,
        )
    fault_local, control_local = sum_both(fault_local, control_local)
    return (adjoint_next[None], window[None], control_local[None], fault_local)


def solution(mesh):
    sub_mesh = Mesh(
        np.asarray(mesh.devices).reshape(SUB_SIZES + (mesh.shape["scen"],)), SUB + ("scen",)
    )
    return jax.shard_map(
        body,
        mesh=sub_mesh,
        in_specs=(
            P(SUB, None, None),
            P(None, SUB, "scen", None),
            P(SUB, "scen", None),
            P(SUB, None),
            P(SUB, None, None),
            P(SUB, None),
            P(SUB, None, None),
            P(SUB, None, None),
            P(SUB, None, None, None, "scen"),
            P(SUB, None),
            P(SUB, None, "scen", None),
            P("scen"),
            P(None, "scen"),
            P(None, "scen"),
        ),
        out_specs=(
            P(SUB, "scen", None),
            P(SUB, None, None, None, "scen"),
            P(SUB, None),
            P("scen"),
        ),
        check_vma=False,
    )
```

```python
import jax
import jax.numpy as jnp
import numpy as np
from jax.sharding import Mesh
from jax.experimental import pallas as pl
from jax.experimental.pallas import tpu as pltpu
from jax import lax
from jax.sharding import PartitionSpec as P

PRECISE = lax.Precision.HIGHEST


SUB = ("z_hi", "x", "y", "core")
SUB_SIZES = (2, 4, 8, 2)


def sum_both(fault_value, control_value):
    for axis in reversed(SUB[1:]):
        fault_value = lax.psum(fault_value, axis)
    fault_mask = (lax.iota(jnp.int32, lax.axis_size("scen")) == lax.axis_index("scen")).astype(
        jnp.float32
    )[:, None]
    control_mask = (lax.iota(jnp.int32, lax.axis_size(SUB[0])) == lax.axis_index(SUB[0])).astype(
        jnp.float32
    )[:, None]
    fault_slots, control_slots = lax.psum(
        (fault_mask * fault_value[None], control_mask * control_value[None]), (SUB[0], "scen")
    )
    return jnp.sum(fault_slots * fault_mask, axis=0), jnp.sum(control_slots * control_mask, axis=0)


def block_scan_kernel(
    grad_ref, picked_ref, table_ref, companion_ref, start_ref, weights_ref, last_ref, samples_ref, inflow_ref, adjoint_ref
):
    steps, scen_rows, node_count = grad_ref.shape
    companion = companion_ref[...]
    inflow_ref[...] = jnp.dot(
        picked_ref[...],
        table_ref[pl.ds(0, picked_ref.shape[1]), :],
        precision=PRECISE,
        preferred_element_type=jnp.float32,
    )

    def one_step(index, adjoint_prev):
        step = steps - 1 - index
        rows = pl.ds(pl.multiple_of(step * scen_rows, scen_rows), scen_rows)
        right_side = grad_ref[step].astype(jnp.float32) + companion * adjoint_prev + inflow_ref[rows]
        adjoint = jnp.dot(
            right_side.astype(jnp.bfloat16), weights_ref[...], preferred_element_type=jnp.float32
        )
        adjoint_ref[rows] = adjoint
        return adjoint

    last_ref[...] = lax.fori_loop(0, steps, one_step, start_ref[...])
    samples_ref[...] = lax.dot_general(
        table_ref[...],
        adjoint_ref[...],
        (((1,), (1,)), ((), ())),
        precision=PRECISE,
        preferred_element_type=jnp.float32,
    )


def block_scan(grad, picked, table, companion, start, weights):
    steps, scen_rows, node_count = grad.shape
    return pl.pallas_call(
        block_scan_kernel,
        out_shape=(
            jax.ShapeDtypeStruct(start.shape, jnp.float32),
            jax.ShapeDtypeStruct((table.shape[0], steps * scen_rows), jnp.float32),
        ),
        scratch_shapes=[
            pltpu.VMEM((steps * scen_rows, node_count), jnp.float32),
            pltpu.VMEM((steps * scen_rows, node_count), jnp.float32),
        ],
    )(grad, picked, table, companion, start, weights)


def passed_along(value, axis, steps):
    count = lax.axis_size(axis)
    pairs = [(source, (source + steps) % count) for source in range(count)]
    return lax.ppermute(value, axis, pairs)


def body(
    inverse_matrix,
    objective_grad,
    final_adjoint,
    companion,
    port_node,
    line_count,
    line_delay,
    line_admittance,
    later_history,
    conv_node,
    conv_drive,
    fault_bus,
    fault_current,
    fault_voltage,
):
    node_count = inverse_matrix.shape[1]
    scen_rows = objective_grad.shape[2]
    slot_count = port_node.shape[2]
    port_total = 4 * slot_count
    conv_count = conv_node.shape[1]
    block_len = later_history.shape[3] // 2
    blocks = objective_grad.shape[0] // block_len
    sub_count = lax.axis_size(SUB)
    grid_width = max(2, sub_count // 16)
    offsets = (1, -1, grid_width, -grid_width)
    opposite = (1, 0, 3, 2)
    sub_index = lax.axis_index(SUB)
    weights = inverse_matrix[0]
    live_mask = (lax.iota(jnp.int32, slot_count)[None, :] < line_count[0][:, None]).astype(
        jnp.float32
    )
    node_iota = lax.iota(jnp.int32, node_count)
    line_scale = (line_admittance[0] * live_mask).reshape(port_total)
    fault_table = (node_iota[None, :] == (fault_bus - sub_index * node_count)[:, None]).astype(
        jnp.float32
    )
    node_table = jnp.concatenate(
        [
            (port_node[0].reshape(port_total)[:, None] == node_iota[None, :]).astype(jnp.float32),
            fault_table,
            (conv_node[0][:, None] == node_iota[None, :]).astype(jnp.float32),
        ],
        axis=0,
    )
    scen_eye = (lax.iota(jnp.int32, scen_rows)[:, None] == lax.iota(jnp.int32, scen_rows)[None, :]).astype(
        jnp.float32
    )
    window = later_history[0]
    adjoint_next = final_adjoint[0]
    control_local = jnp.zeros((conv_count,), jnp.float32)
    fault_local = jnp.zeros((scen_rows,), jnp.float32)
    block_rows = lax.iota(jnp.int32, block_len)
    time_iota = lax.iota(jnp.int32, 2 * block_len)


    for block_id in reversed(range(blocks)):
        block_start = block_id * block_len
        target = block_rows[None, None, :] + line_delay[0][:, :, None] - block_len
        time_table = (target[..., None] == time_iota).astype(jnp.float32)
        picked = jnp.concatenate(
            [
                jnp.einsum("ecji,ecis->jsec", time_table, window, precision=PRECISE).reshape(
                    block_len * scen_rows, port_total
                )
                * line_scale[None, :],
                (fault_current[block_start : block_start + block_len, :, None] * scen_eye[None]).reshape(
                    block_len * scen_rows, scen_rows
                ),
            ],
            axis=1,
        )
        adjoint_next, samples = block_scan(
            objective_grad[block_start : block_start + block_len, 0],
            picked,
            node_table,
            companion,
            adjoint_next,
            weights,
        )
        samples = lax.optimization_barrier(samples)
        outbound = samples[:port_total].reshape(4, slot_count, block_len * scen_rows) * live_mask[
            :, :, None
        ]
        at_fault = jnp.sum(
            samples[port_total : port_total + scen_rows].reshape(scen_rows, block_len, scen_rows)
            * scen_eye[:, None, :],
            axis=0,
        )
        fault_term = jnp.sum(at_fault * fault_voltage[block_start : block_start + block_len], axis=0)
        at_conv = samples[port_total + scen_rows :].reshape(conv_count, block_len, scen_rows)
        control_term = jnp.sum(
            at_conv * jnp.transpose(conv_drive[0, block_start : block_start + block_len], (2, 0, 1)),
            axis=(1, 2),
        )
        control_local = control_local + control_term
        fault_local = fault_local + fault_term
        received = jnp.stack(
            [
                passed_along(outbound[opposite[direction]], SUB, -offsets[direction])
                for direction in range(4)
            ]
        )
        received, fault_local, control_local = lax.optimization_barrier(
            (received, fault_local, control_local)
        )
        window = jnp.concatenate(
            [received.reshape(4, slot_count, block_len, scen_rows), window[:, :, :block_len]],
            axis=2,
        )
    fault_local, control_local = sum_both(fault_local, control_local)
    return (adjoint_next[None], window[None], control_local[None], fault_local)


def solution(mesh):
    sub_mesh = Mesh(
        np.asarray(mesh.devices).reshape(SUB_SIZES + (mesh.shape["scen"],)), SUB + ("scen",)
    )
    return jax.shard_map(
        body,
        mesh=sub_mesh,
        in_specs=(
            P(SUB, None, None),
            P(None, SUB, "scen", None),
            P(SUB, "scen", None),
            P(SUB, None),
            P(SUB, None, None),
            P(SUB, None),
            P(SUB, None, None),
            P(SUB, None, None),
            P(SUB, None, None, None, "scen"),
            P(SUB, None),
            P(SUB, None, "scen", None),
            P("scen"),
            P(None, "scen"),
            P(None, "scen"),
        ),
        out_specs=(
            P(SUB, "scen", None),
            P(SUB, None, None, None, "scen"),
            P(SUB, None),
            P("scen"),
        ),
        check_vma=False,
    )
```

```python
import functools

import jax
import jax.numpy as jnp
import numpy as np
from jax.sharding import Mesh
from jax.experimental import pallas as pl
from jax.experimental.pallas import tpu as pltpu
from jax import lax
from jax.sharding import PartitionSpec as P

PRECISE = lax.Precision.HIGHEST


SUB = ("z_hi", "x", "y", "core")
SUB_SIZES = (2, 4, 8, 2)


def sum_both(fault_value, control_value):
    for axis in reversed(SUB[1:]):
        fault_value = lax.psum(fault_value, axis)
    fault_mask = (lax.iota(jnp.int32, lax.axis_size("scen")) == lax.axis_index("scen")).astype(
        jnp.float32
    )[:, None]
    control_mask = (lax.iota(jnp.int32, lax.axis_size(SUB[0])) == lax.axis_index(SUB[0])).astype(
        jnp.float32
    )[:, None]
    fault_slots, control_slots = lax.psum(
        (fault_mask * fault_value[None], control_mask * control_value[None]), (SUB[0], "scen")
    )
    return jnp.sum(fault_slots * fault_mask, axis=0), jnp.sum(control_slots * control_mask, axis=0)


def block_scan_kernel(
    block_start,
    grad_ref,
    picked_ref,
    spread_ref,
    companion_ref,
    start_ref,
    weights_ref,
    pick_ref,
    voltage_ref,
    last_ref,
    samples_ref,
    fault_out_ref,
    inflow_ref,
    adjoint_ref,
):
    steps, scen_rows, node_count = grad_ref.shape
    companion = companion_ref[...]
    inflow_ref[...] = jnp.dot(
        picked_ref[...], spread_ref[...], precision=PRECISE, preferred_element_type=jnp.float32
    )

    def one_step(index, adjoint_prev):
        step = steps - 1 - index
        rows = pl.ds(pl.multiple_of(step * scen_rows, scen_rows), scen_rows)
        right_side = (
            grad_ref[step].astype(jnp.float32)
            + companion * adjoint_prev
            + inflow_ref[rows]
        )
        adjoint = jnp.dot(
            right_side.astype(jnp.bfloat16), weights_ref[...], preferred_element_type=jnp.float32
        )
        adjoint_ref[rows] = adjoint
        return adjoint

    last_ref[...] = lax.fori_loop(0, steps, one_step, start_ref[...])
    adjoint_block = adjoint_ref[...]
    samples_ref[...] = jnp.dot(
        adjoint_block, pick_ref[...], precision=PRECISE, preferred_element_type=jnp.float32
    )
    fault_table = spread_ref[pl.ds(spread_ref.shape[0] - scen_rows, scen_rows), :]
    at_fault = jnp.sum(adjoint_block.reshape(steps, scen_rows, node_count) * fault_table[None], axis=2)
    voltage = voltage_ref[pl.ds(block_start, steps), :]
    fault_out_ref[...] = jnp.sum(at_fault * voltage, axis=0, keepdims=True)


def block_scan(block_start, grad, picked, spread, companion, start, weights, pick, voltage):
    steps, scen_rows, node_count = grad.shape
    return pl.pallas_call(
        functools.partial(block_scan_kernel, block_start),
        out_shape=(
            jax.ShapeDtypeStruct(start.shape, jnp.float32),
            jax.ShapeDtypeStruct((steps * scen_rows, pick.shape[1]), jnp.float32),
            jax.ShapeDtypeStruct((1, scen_rows), jnp.float32),
        ),
        scratch_shapes=[
            pltpu.VMEM((steps * scen_rows, node_count), jnp.float32),
            pltpu.VMEM((steps * scen_rows, node_count), jnp.float32),
        ],
    )(grad, picked, spread, companion, start, weights, pick, voltage)


def passed_along(value, axis, steps):
    count = lax.axis_size(axis)
    pairs = [(source, (source + steps) % count) for source in range(count)]
    return lax.ppermute(value, axis, pairs)


def body(
    inverse_matrix,
    objective_grad,
    final_adjoint,
    companion,
    port_node,
    line_count,
    line_delay,
    line_admittance,
    later_history,
    conv_node,
    conv_drive,
    fault_bus,
    fault_current,
    fault_voltage,
):
    node_count = inverse_matrix.shape[1]
    scen_rows = objective_grad.shape[2]
    slot_count = port_node.shape[2]
    port_total = 4 * slot_count
    conv_count = conv_node.shape[1]
    block_len = later_history.shape[3] // 2
    blocks = objective_grad.shape[0] // block_len
    sub_count = lax.axis_size(SUB)
    grid_width = max(2, sub_count // 16)
    offsets = (1, -1, grid_width, -grid_width)
    opposite = (1, 0, 3, 2)
    sub_index = lax.axis_index(SUB)
    weights = inverse_matrix[0]
    live_mask = (lax.iota(jnp.int32, slot_count)[None, :] < line_count[0][:, None]).astype(
        jnp.float32
    )
    node_iota = lax.iota(jnp.int32, node_count)
    pick_table = jnp.concatenate(
        [
            node_iota[:, None] == port_node[0].reshape(port_total)[None, :],
            node_iota[:, None] == conv_node[0][None, :],
        ],
        axis=1,
    ).astype(jnp.float32)
    line_scale = (line_admittance[0] * live_mask).reshape(port_total)
    fault_table = (node_iota[None, :] == (fault_bus - sub_index * node_count)[:, None]).astype(
        jnp.float32
    )
    spread_table = jnp.concatenate(
        [
            (port_node[0].reshape(port_total)[:, None] == node_iota[None, :]).astype(jnp.float32),
            fault_table,
        ],
        axis=0,
    )
    scen_eye = (lax.iota(jnp.int32, scen_rows)[:, None] == lax.iota(jnp.int32, scen_rows)[None, :]).astype(
        jnp.float32
    )
    window = later_history[0]
    adjoint_next = final_adjoint[0]
    control_local = jnp.zeros((conv_count,), jnp.float32)
    fault_local = jnp.zeros((scen_rows,), jnp.float32)
    block_rows = lax.iota(jnp.int32, block_len)
    time_iota = lax.iota(jnp.int32, 2 * block_len)


    for block_id in reversed(range(blocks)):
        block_start = block_id * block_len
        target = block_rows[None, None, :] + line_delay[0][:, :, None] - block_len
        time_table = (target[..., None] == time_iota).astype(jnp.float32)
        picked = jnp.concatenate(
            [
                jnp.einsum("ecji,ecis->jsec", time_table, window, precision=PRECISE).reshape(
                    block_len * scen_rows, port_total
                )
                * line_scale[None, :],
                (fault_current[block_start : block_start + block_len, :, None] * scen_eye[None]).reshape(
                    block_len * scen_rows, scen_rows
                ),
            ],
            axis=1,
        )
        adjoint_next, samples, fault_term = block_scan(
            block_start,
            objective_grad[block_start : block_start + block_len, 0],
            picked,
            spread_table,
            companion,
            adjoint_next,
            weights,
            pick_table,
            fault_voltage,
        )
        samples, fault_term = lax.optimization_barrier((samples, fault_term[0]))
        series = (
            jnp.transpose(
                samples[:, :port_total].reshape(block_len, scen_rows, 4, slot_count), (2, 3, 0, 1)
            )
            * live_mask[:, :, None, None]
        )
        outbound = series.reshape(4, slot_count, block_len * scen_rows)
        control_term = jnp.sum(
            samples[:, port_total:].reshape(block_len, scen_rows, conv_count)
            * conv_drive[0, block_start : block_start + block_len],
            axis=(0, 1),
        )
        control_local = control_local + control_term
        fault_local = fault_local + fault_term
        received = jnp.stack(
            [
                passed_along(outbound[opposite[direction]], SUB, -offsets[direction])
                for direction in range(4)
            ]
        )
        window = jnp.concatenate(
            [received.reshape(4, slot_count, block_len, scen_rows), window[:, :, :block_len]],
            axis=2,
        )
    fault_local, control_local = sum_both(fault_local, control_local)
    return (adjoint_next[None], window[None], control_local[None], fault_local)


def solution(mesh):
    sub_mesh = Mesh(
        np.asarray(mesh.devices).reshape(SUB_SIZES + (mesh.shape["scen"],)), SUB + ("scen",)
    )
    return jax.shard_map(
        body,
        mesh=sub_mesh,
        in_specs=(
            P(SUB, None, None),
            P(None, SUB, "scen", None),
            P(SUB, "scen", None),
            P(SUB, None),
            P(SUB, None, None),
            P(SUB, None),
            P(SUB, None, None),
            P(SUB, None, None),
            P(SUB, None, None, None, "scen"),
            P(SUB, None),
            P(SUB, None, "scen", None),
            P("scen"),
            P(None, "scen"),
            P(None, "scen"),
        ),
        out_specs=(
            P(SUB, "scen", None),
            P(SUB, None, None, None, "scen"),
            P(SUB, None),
            P("scen"),
        ),
        check_vma=False,
    )
```

```python
import functools

import jax
import jax.numpy as jnp
import numpy as np
from jax.sharding import Mesh
from jax.experimental import pallas as pl
from jax.experimental.pallas import tpu as pltpu
from jax import lax
from jax.sharding import PartitionSpec as P

PRECISE = lax.Precision.HIGHEST


SUB = ("z_hi", "x", "y", "core")
SUB_SIZES = (2, 4, 8, 2)


def sum_both(fault_value, control_value):
    for axis in reversed(SUB[1:]):
        fault_value = lax.psum(fault_value, axis)
    fault_mask = (lax.iota(jnp.int32, lax.axis_size("scen")) == lax.axis_index("scen")).astype(
        jnp.float32
    )[:, None]
    control_mask = (lax.iota(jnp.int32, lax.axis_size(SUB[0])) == lax.axis_index(SUB[0])).astype(
        jnp.float32
    )[:, None]
    fault_slots, control_slots = lax.psum(
        (fault_mask * fault_value[None], control_mask * control_value[None]), (SUB[0], "scen")
    )
    return jnp.sum(fault_slots * fault_mask, axis=0), jnp.sum(control_slots * control_mask, axis=0)


def block_scan_kernel(
    block_start,
    grad_ref,
    picked_ref,
    spread_ref,
    companion_ref,
    start_ref,
    weights_ref,
    pick_ref,
    voltage_ref,
    last_ref,
    samples_ref,
    fault_out_ref,
    inflow_ref,
    adjoint_ref,
):
    steps, scen_rows, node_count = grad_ref.shape
    companion = companion_ref[...]
    inflow_ref[...] = jnp.dot(
        picked_ref[...], spread_ref[...], precision=PRECISE, preferred_element_type=jnp.float32
    )

    def one_step(index, adjoint_prev):
        step = steps - 1 - index
        rows = pl.ds(pl.multiple_of(step * scen_rows, scen_rows), scen_rows)
        right_side = (
            grad_ref[step].astype(jnp.float32)
            + companion * adjoint_prev
            + inflow_ref[rows]
        )
        adjoint = jnp.dot(
            right_side.astype(jnp.bfloat16), weights_ref[...], preferred_element_type=jnp.float32
        )
        adjoint_ref[rows] = adjoint
        return adjoint

    last_ref[...] = lax.fori_loop(0, steps, one_step, start_ref[...])
    adjoint_block = adjoint_ref[...]
    samples_ref[...] = jnp.dot(
        adjoint_block, pick_ref[...], precision=PRECISE, preferred_element_type=jnp.float32
    )
    fault_table = spread_ref[pl.ds(spread_ref.shape[0] - scen_rows, scen_rows), :]
    at_fault = jnp.sum(adjoint_block.reshape(steps, scen_rows, node_count) * fault_table[None], axis=2)
    voltage = voltage_ref[pl.ds(block_start, steps), :]
    fault_out_ref[...] = jnp.sum(at_fault * voltage, axis=0, keepdims=True)


def whole(array):
    return pl.BlockSpec(array.shape, lambda index: (0,) * array.ndim)


def block_scan(block_start, steps, grad, picked, spread, companion, start, weights, pick, voltage):
    _, _, scen_rows, node_count = grad.shape
    block_id = block_start // steps
    operands = (grad, picked, spread, companion, start, weights, pick, voltage)
    return pl.pallas_call(
        functools.partial(block_scan_kernel, block_start),
        grid=(1,),
        in_specs=[
            pl.BlockSpec(
                (steps, None, scen_rows, node_count), lambda index: (block_id, 0, 0, 0)
            )
        ]
        + [whole(array) for array in operands[1:]],
        out_specs=(
            whole(start),
            pl.BlockSpec((steps * scen_rows, pick.shape[1]), lambda index: (0, 0)),
            pl.BlockSpec((1, scen_rows), lambda index: (0, 0)),
        ),
        out_shape=(
            jax.ShapeDtypeStruct(start.shape, jnp.float32),
            jax.ShapeDtypeStruct((steps * scen_rows, pick.shape[1]), jnp.float32),
            jax.ShapeDtypeStruct((1, scen_rows), jnp.float32),
        ),
        scratch_shapes=[
            pltpu.VMEM((steps * scen_rows, node_count), jnp.float32),
            pltpu.VMEM((steps * scen_rows, node_count), jnp.float32),
        ],
    )(*operands)


def passed_along(value, axis, steps):
    count = lax.axis_size(axis)
    pairs = [(source, (source + steps) % count) for source in range(count)]
    return lax.ppermute(value, axis, pairs)


def body(
    inverse_matrix,
    objective_grad,
    final_adjoint,
    companion,
    port_node,
    line_count,
    line_delay,
    line_admittance,
    later_history,
    conv_node,
    conv_drive,
    fault_bus,
    fault_current,
    fault_voltage,
):
    node_count = inverse_matrix.shape[1]
    scen_rows = objective_grad.shape[2]
    slot_count = port_node.shape[2]
    port_total = 4 * slot_count
    conv_count = conv_node.shape[1]
    block_len = later_history.shape[3] // 2
    blocks = objective_grad.shape[0] // block_len
    sub_count = lax.axis_size(SUB)
    grid_width = max(2, sub_count // 16)
    offsets = (1, -1, grid_width, -grid_width)
    opposite = (1, 0, 3, 2)
    sub_index = lax.axis_index(SUB)
    weights = inverse_matrix[0]
    live_mask = (lax.iota(jnp.int32, slot_count)[None, :] < line_count[0][:, None]).astype(
        jnp.float32
    )
    node_iota = lax.iota(jnp.int32, node_count)
    pick_table = jnp.concatenate(
        [
            node_iota[:, None] == port_node[0].reshape(port_total)[None, :],
            node_iota[:, None] == conv_node[0][None, :],
        ],
        axis=1,
    ).astype(jnp.float32)
    line_scale = (line_admittance[0] * live_mask).reshape(port_total)
    fault_table = (node_iota[None, :] == (fault_bus - sub_index * node_count)[:, None]).astype(
        jnp.float32
    )
    spread_table = jnp.concatenate(
        [
            (port_node[0].reshape(port_total)[:, None] == node_iota[None, :]).astype(jnp.float32),
            fault_table,
        ],
        axis=0,
    )
    scen_eye = (lax.iota(jnp.int32, scen_rows)[:, None] == lax.iota(jnp.int32, scen_rows)[None, :]).astype(
        jnp.float32
    )
    window = later_history[0]
    adjoint_next = final_adjoint[0]
    control_local = jnp.zeros((conv_count,), jnp.float32)
    fault_local = jnp.zeros((scen_rows,), jnp.float32)
    block_rows = lax.iota(jnp.int32, block_len)
    time_iota = lax.iota(jnp.int32, 2 * block_len)


    for block_id in reversed(range(blocks)):
        block_start = block_id * block_len
        target = block_rows[None, None, :] + line_delay[0][:, :, None] - block_len
        time_table = (target[..., None] == time_iota).astype(jnp.float32)
        picked = jnp.concatenate(
            [
                jnp.einsum("ecji,ecis->jsec", time_table, window, precision=PRECISE).reshape(
                    block_len * scen_rows, port_total
                )
                * line_scale[None, :],
                (fault_current[block_start : block_start + block_len, :, None] * scen_eye[None]).reshape(
                    block_len * scen_rows, scen_rows
                ),
            ],
            axis=1,
        )
        adjoint_next, samples, fault_term = block_scan(
            block_start,
            block_len,
            objective_grad,
            picked,
            spread_table,
            companion,
            adjoint_next,
            weights,
            pick_table,
            fault_voltage,
        )
        samples, fault_term = lax.optimization_barrier((samples, fault_term[0]))
        series = (
            jnp.transpose(
                samples[:, :port_total].reshape(block_len, scen_rows, 4, slot_count), (2, 3, 0, 1)
            )
            * live_mask[:, :, None, None]
        )
        outbound = series.reshape(4, slot_count, block_len * scen_rows)
        control_term = jnp.sum(
            samples[:, port_total:].reshape(block_len, scen_rows, conv_count)
            * conv_drive[0, block_start : block_start + block_len],
            axis=(0, 1),
        )
        control_local = control_local + control_term
        fault_local = fault_local + fault_term
        received = jnp.stack(
            [
                passed_along(outbound[opposite[direction]], SUB, -offsets[direction])
                for direction in range(4)
            ]
        )
        window = jnp.concatenate(
            [received.reshape(4, slot_count, block_len, scen_rows), window[:, :, :block_len]],
            axis=2,
        )
    fault_local, control_local = sum_both(fault_local, control_local)
    return (adjoint_next[None], window[None], control_local[None], fault_local)


def solution(mesh):
    sub_mesh = Mesh(
        np.asarray(mesh.devices).reshape(SUB_SIZES + (mesh.shape["scen"],)), SUB + ("scen",)
    )
    return jax.shard_map(
        body,
        mesh=sub_mesh,
        in_specs=(
            P(SUB, None, None),
            P(None, SUB, "scen", None),
            P(SUB, "scen", None),
            P(SUB, None),
            P(SUB, None, None),
            P(SUB, None),
            P(SUB, None, None),
            P(SUB, None, None),
            P(SUB, None, None, None, "scen"),
            P(SUB, None),
            P(SUB, None, "scen", None),
            P("scen"),
            P(None, "scen"),
            P(None, "scen"),
        ),
        out_specs=(
            P(SUB, "scen", None),
            P(SUB, None, None, None, "scen"),
            P(SUB, None),
            P("scen"),
        ),
        check_vma=False,
    )
```

```python
import functools

import jax
import jax.numpy as jnp
import numpy as np
from jax.sharding import Mesh
from jax.experimental import pallas as pl
from jax.experimental.pallas import tpu as pltpu
from jax import lax
from jax.sharding import PartitionSpec as P

PRECISE = lax.Precision.HIGHEST


SUB = ("z_hi", "x", "y", "core")
SUB_SIZES = (2, 4, 8, 2)


def sum_both(fault_value, control_value):
    for axis in reversed(SUB[1:]):
        fault_value = lax.psum(fault_value, axis)
    fault_mask = (lax.iota(jnp.int32, lax.axis_size("scen")) == lax.axis_index("scen")).astype(
        jnp.float32
    )[:, None]
    control_mask = (lax.iota(jnp.int32, lax.axis_size(SUB[0])) == lax.axis_index(SUB[0])).astype(
        jnp.float32
    )[:, None]
    fault_slots, control_slots = lax.psum(
        (fault_mask * fault_value[None], control_mask * control_value[None]), (SUB[0], "scen")
    )
    return jnp.sum(fault_slots * fault_mask, axis=0), jnp.sum(control_slots * control_mask, axis=0)


def block_scan_kernel(
    block_start,
    grad_ref,
    picked_ref,
    spread_ref,
    companion_ref,
    start_ref,
    weights_ref,
    pick_ref,
    voltage_ref,
    last_ref,
    samples_ref,
    fault_out_ref,
    inflow_ref,
    adjoint_ref,
):
    steps, scen_rows, node_count = grad_ref.shape
    companion = companion_ref[...]
    inflow_ref[...] = jnp.dot(
        picked_ref[...], spread_ref[...], precision=PRECISE, preferred_element_type=jnp.float32
    )

    def one_step(index, adjoint_prev):
        step = steps - 1 - index
        rows = pl.ds(pl.multiple_of(step * scen_rows, scen_rows), scen_rows)
        right_side = (
            grad_ref[step].astype(jnp.float32)
            + companion * adjoint_prev
            + inflow_ref[rows]
        )
        adjoint = jnp.dot(
            right_side.astype(jnp.bfloat16), weights_ref[...], preferred_element_type=jnp.float32
        )
        adjoint_ref[rows] = adjoint
        return adjoint

    last_ref[...] = lax.fori_loop(0, steps, one_step, start_ref[...], unroll=True)
    adjoint_block = adjoint_ref[...]
    samples_ref[...] = jnp.dot(
        adjoint_block, pick_ref[...], precision=PRECISE, preferred_element_type=jnp.float32
    )
    fault_table = spread_ref[pl.ds(spread_ref.shape[0] - scen_rows, scen_rows), :]
    at_fault = jnp.sum(adjoint_block.reshape(steps, scen_rows, node_count) * fault_table[None], axis=2)
    voltage = voltage_ref[pl.ds(block_start, steps), :]
    fault_out_ref[...] = jnp.sum(at_fault * voltage, axis=0, keepdims=True)


def whole(array):
    return pl.BlockSpec(array.shape, lambda index: (0,) * array.ndim)


def block_scan(block_start, steps, grad, picked, spread, companion, start, weights, pick, voltage):
    _, _, scen_rows, node_count = grad.shape
    block_id = block_start // steps
    operands = (grad, picked, spread, companion, start, weights, pick, voltage)
    return pl.pallas_call(
        functools.partial(block_scan_kernel, block_start),
        grid=(1,),
        in_specs=[
            pl.BlockSpec(
                (steps, None, scen_rows, node_count), lambda index: (block_id, 0, 0, 0)
            )
        ]
        + [whole(array) for array in operands[1:]],
        out_specs=(
            whole(start),
            pl.BlockSpec((steps * scen_rows, pick.shape[1]), lambda index: (0, 0)),
            pl.BlockSpec((1, scen_rows), lambda index: (0, 0)),
        ),
        out_shape=(
            jax.ShapeDtypeStruct(start.shape, jnp.float32),
            jax.ShapeDtypeStruct((steps * scen_rows, pick.shape[1]), jnp.float32),
            jax.ShapeDtypeStruct((1, scen_rows), jnp.float32),
        ),
        scratch_shapes=[
            pltpu.VMEM((steps * scen_rows, node_count), jnp.float32),
            pltpu.VMEM((steps * scen_rows, node_count), jnp.float32),
        ],
    )(*operands)


def passed_along(value, axis, steps):
    count = lax.axis_size(axis)
    pairs = [(source, (source + steps) % count) for source in range(count)]
    return lax.ppermute(value, axis, pairs)


def body(
    inverse_matrix,
    objective_grad,
    final_adjoint,
    companion,
    port_node,
    line_count,
    line_delay,
    line_admittance,
    later_history,
    conv_node,
    conv_drive,
    fault_bus,
    fault_current,
    fault_voltage,
):
    node_count = inverse_matrix.shape[1]
    scen_rows = objective_grad.shape[2]
    slot_count = port_node.shape[2]
    port_total = 4 * slot_count
    conv_count = conv_node.shape[1]
    block_len = later_history.shape[3] // 2
    blocks = objective_grad.shape[0] // block_len
    sub_count = lax.axis_size(SUB)
    grid_width = max(2, sub_count // 16)
    offsets = (1, -1, grid_width, -grid_width)
    opposite = (1, 0, 3, 2)
    sub_index = lax.axis_index(SUB)
    weights = inverse_matrix[0]
    live_mask = (lax.iota(jnp.int32, slot_count)[None, :] < line_count[0][:, None]).astype(
        jnp.float32
    )
    node_iota = lax.iota(jnp.int32, node_count)
    pick_table = jnp.concatenate(
        [
            node_iota[:, None] == port_node[0].reshape(port_total)[None, :],
            node_iota[:, None] == conv_node[0][None, :],
        ],
        axis=1,
    ).astype(jnp.float32)
    line_scale = (line_admittance[0] * live_mask).reshape(port_total)
    fault_table = (node_iota[None, :] == (fault_bus - sub_index * node_count)[:, None]).astype(
        jnp.float32
    )
    spread_table = jnp.concatenate(
        [
            (port_node[0].reshape(port_total)[:, None] == node_iota[None, :]).astype(jnp.float32),
            fault_table,
        ],
        axis=0,
    )
    scen_eye = (lax.iota(jnp.int32, scen_rows)[:, None] == lax.iota(jnp.int32, scen_rows)[None, :]).astype(
        jnp.float32
    )
    window = later_history[0]
    adjoint_next = final_adjoint[0]
    control_local = jnp.zeros((conv_count,), jnp.float32)
    fault_local = jnp.zeros((scen_rows,), jnp.float32)
    block_rows = lax.iota(jnp.int32, block_len)
    time_iota = lax.iota(jnp.int32, 2 * block_len)


    for block_id in reversed(range(blocks)):
        block_start = block_id * block_len
        target = block_rows[None, None, :] + line_delay[0][:, :, None] - block_len
        time_table = (target[..., None] == time_iota).astype(jnp.float32)
        picked = jnp.concatenate(
            [
                jnp.einsum("ecji,ecis->jsec", time_table, window, precision=PRECISE).reshape(
                    block_len * scen_rows, port_total
                )
                * line_scale[None, :],
                (fault_current[block_start : block_start + block_len, :, None] * scen_eye[None]).reshape(
                    block_len * scen_rows, scen_rows
                ),
            ],
            axis=1,
        )
        adjoint_next, samples, fault_term = block_scan(
            block_start,
            block_len,
            objective_grad,
            picked,
            spread_table,
            companion,
            adjoint_next,
            weights,
            pick_table,
            fault_voltage,
        )
        samples, fault_term = lax.optimization_barrier((samples, fault_term[0]))
        series = (
            jnp.transpose(
                samples[:, :port_total].reshape(block_len, scen_rows, 4, slot_count), (2, 3, 0, 1)
            )
            * live_mask[:, :, None, None]
        )
        outbound = series.reshape(4, slot_count, block_len * scen_rows)
        control_term = jnp.sum(
            samples[:, port_total:].reshape(block_len, scen_rows, conv_count)
            * conv_drive[0, block_start : block_start + block_len],
            axis=(0, 1),
        )
        control_local = control_local + control_term
        fault_local = fault_local + fault_term
        received = jnp.stack(
            [
                passed_along(outbound[opposite[direction]], SUB, -offsets[direction])
                for direction in range(4)
            ]
        )
        window = jnp.concatenate(
            [received.reshape(4, slot_count, block_len, scen_rows), window[:, :, :block_len]],
            axis=2,
        )
    fault_local, control_local = sum_both(fault_local, control_local)
    return (adjoint_next[None], window[None], control_local[None], fault_local)


def solution(mesh):
    sub_mesh = Mesh(
        np.asarray(mesh.devices).reshape(SUB_SIZES + (mesh.shape["scen"],)), SUB + ("scen",)
    )
    return jax.shard_map(
        body,
        mesh=sub_mesh,
        in_specs=(
            P(SUB, None, None),
            P(None, SUB, "scen", None),
            P(SUB, "scen", None),
            P(SUB, None),
            P(SUB, None, None),
            P(SUB, None),
            P(SUB, None, None),
            P(SUB, None, None),
            P(SUB, None, None, None, "scen"),
            P(SUB, None),
            P(SUB, None, "scen", None),
            P("scen"),
            P(None, "scen"),
            P(None, "scen"),
        ),
        out_specs=(
            P(SUB, "scen", None),
            P(SUB, None, None, None, "scen"),
            P(SUB, None),
            P("scen"),
        ),
        check_vma=False,
    )
```

```python
import functools

import jax
import jax.numpy as jnp
import numpy as np
from jax.sharding import Mesh
from jax.experimental import pallas as pl
from jax.experimental.pallas import tpu as pltpu
from jax import lax
from jax.sharding import PartitionSpec as P

PRECISE = lax.Precision.HIGHEST


SUB = ("z_hi", "x", "y", "core")
SUB_SIZES = (2, 4, 8, 2)


def sum_both(fault_value, control_value):
    for axis in reversed(SUB[1:]):
        fault_value = lax.psum(fault_value, axis)
    fault_mask = (lax.iota(jnp.int32, lax.axis_size("scen")) == lax.axis_index("scen")).astype(
        jnp.float32
    )[:, None]
    control_mask = (lax.iota(jnp.int32, lax.axis_size(SUB[0])) == lax.axis_index(SUB[0])).astype(
        jnp.float32
    )[:, None]
    fault_slots, control_slots = lax.psum(
        (fault_mask * fault_value[None], control_mask * control_value[None]), (SUB[0], "scen")
    )
    return jnp.sum(fault_slots * fault_mask, axis=0), jnp.sum(control_slots * control_mask, axis=0)


def block_scan_kernel(
    block_start,
    grad_ref,
    picked_ref,
    spread_ref,
    companion_ref,
    start_ref,
    weights_ref,
    pick_ref,
    voltage_ref,
    last_ref,
    samples_ref,
    fault_out_ref,
    inflow_ref,
    adjoint_ref,
):
    steps, scen_rows, node_count = grad_ref.shape
    companion = companion_ref[...]
    inflow_ref[...] = jnp.dot(
        picked_ref[...], spread_ref[...], precision=lax.Precision.HIGH, preferred_element_type=jnp.float32
    )

    def one_step(index, adjoint_prev):
        step = steps - 1 - index
        rows = pl.ds(pl.multiple_of(step * scen_rows, scen_rows), scen_rows)
        right_side = (
            grad_ref[step].astype(jnp.float32)
            + companion * adjoint_prev
            + inflow_ref[rows]
        )
        adjoint = jnp.dot(
            right_side.astype(jnp.bfloat16), weights_ref[...], preferred_element_type=jnp.float32
        )
        adjoint_ref[rows] = adjoint
        return adjoint

    last_ref[...] = lax.fori_loop(0, steps, one_step, start_ref[...], unroll=True)
    adjoint_block = adjoint_ref[...]
    samples_ref[...] = jnp.dot(
        adjoint_block, pick_ref[...], precision=lax.Precision.HIGH, preferred_element_type=jnp.float32
    )
    fault_table = spread_ref[pl.ds(spread_ref.shape[0] - scen_rows, scen_rows), :]
    at_fault = jnp.sum(adjoint_block.reshape(steps, scen_rows, node_count) * fault_table[None], axis=2)
    voltage = voltage_ref[pl.ds(block_start, steps), :]
    fault_out_ref[...] = jnp.sum(at_fault * voltage, axis=0, keepdims=True)


def whole(array):
    return pl.BlockSpec(array.shape, lambda index: (0,) * array.ndim)


def block_scan(block_start, steps, grad, picked, spread, companion, start, weights, pick, voltage):
    _, _, scen_rows, node_count = grad.shape
    block_id = block_start // steps
    operands = (grad, picked, spread, companion, start, weights, pick, voltage)
    return pl.pallas_call(
        functools.partial(block_scan_kernel, block_start),
        grid=(1,),
        in_specs=[
            pl.BlockSpec(
                (steps, None, scen_rows, node_count), lambda index: (block_id, 0, 0, 0)
            )
        ]
        + [whole(array) for array in operands[1:]],
        out_specs=(
            whole(start),
            pl.BlockSpec((steps * scen_rows, pick.shape[1]), lambda index: (0, 0)),
            pl.BlockSpec((1, scen_rows), lambda index: (0, 0)),
        ),
        out_shape=(
            jax.ShapeDtypeStruct(start.shape, jnp.float32),
            jax.ShapeDtypeStruct((steps * scen_rows, pick.shape[1]), jnp.float32),
            jax.ShapeDtypeStruct((1, scen_rows), jnp.float32),
        ),
        scratch_shapes=[
            pltpu.VMEM((steps * scen_rows, node_count), jnp.float32),
            pltpu.VMEM((steps * scen_rows, node_count), jnp.float32),
        ],
    )(*operands)


def passed_along(value, axis, steps):
    count = lax.axis_size(axis)
    pairs = [(source, (source + steps) % count) for source in range(count)]
    return lax.ppermute(value, axis, pairs)


def body(
    inverse_matrix,
    objective_grad,
    final_adjoint,
    companion,
    port_node,
    line_count,
    line_delay,
    line_admittance,
    later_history,
    conv_node,
    conv_drive,
    fault_bus,
    fault_current,
    fault_voltage,
):
    node_count = inverse_matrix.shape[1]
    scen_rows = objective_grad.shape[2]
    slot_count = port_node.shape[2]
    port_total = 4 * slot_count
    conv_count = conv_node.shape[1]
    block_len = later_history.shape[3] // 2
    blocks = objective_grad.shape[0] // block_len
    sub_count = lax.axis_size(SUB)
    grid_width = max(2, sub_count // 16)
    offsets = (1, -1, grid_width, -grid_width)
    opposite = (1, 0, 3, 2)
    sub_index = lax.axis_index(SUB)
    weights = inverse_matrix[0]
    live_mask = (lax.iota(jnp.int32, slot_count)[None, :] < line_count[0][:, None]).astype(
        jnp.float32
    )
    node_iota = lax.iota(jnp.int32, node_count)
    pick_table = jnp.concatenate(
        [
            node_iota[:, None] == port_node[0].reshape(port_total)[None, :],
            node_iota[:, None] == conv_node[0][None, :],
        ],
        axis=1,
    ).astype(jnp.float32)
    line_scale = (line_admittance[0] * live_mask).reshape(port_total)
    fault_table = (node_iota[None, :] == (fault_bus - sub_index * node_count)[:, None]).astype(
        jnp.float32
    )
    spread_table = jnp.concatenate(
        [
            (port_node[0].reshape(port_total)[:, None] == node_iota[None, :]).astype(jnp.float32),
            fault_table,
        ],
        axis=0,
    )
    scen_eye = (lax.iota(jnp.int32, scen_rows)[:, None] == lax.iota(jnp.int32, scen_rows)[None, :]).astype(
        jnp.float32
    )
    window = later_history[0]
    adjoint_next = final_adjoint[0]
    control_local = jnp.zeros((conv_count,), jnp.float32)
    fault_local = jnp.zeros((scen_rows,), jnp.float32)
    block_rows = lax.iota(jnp.int32, block_len)
    time_iota = lax.iota(jnp.int32, 2 * block_len)


    for block_id in reversed(range(blocks)):
        block_start = block_id * block_len
        target = block_rows[None, None, :] + line_delay[0][:, :, None] - block_len
        time_table = (target[..., None] == time_iota).astype(jnp.float32)
        picked = jnp.concatenate(
            [
                jnp.einsum("ecji,ecis->jsec", time_table, window, precision=PRECISE).reshape(
                    block_len * scen_rows, port_total
                )
                * line_scale[None, :],
                (fault_current[block_start : block_start + block_len, :, None] * scen_eye[None]).reshape(
                    block_len * scen_rows, scen_rows
                ),
            ],
            axis=1,
        )
        adjoint_next, samples, fault_term = block_scan(
            block_start,
            block_len,
            objective_grad,
            picked,
            spread_table,
            companion,
            adjoint_next,
            weights,
            pick_table,
            fault_voltage,
        )
        samples, fault_term = lax.optimization_barrier((samples, fault_term[0]))
        series = (
            jnp.transpose(
                samples[:, :port_total].reshape(block_len, scen_rows, 4, slot_count), (2, 3, 0, 1)
            )
            * live_mask[:, :, None, None]
        )
        outbound = series.reshape(4, slot_count, block_len * scen_rows)
        control_term = jnp.sum(
            samples[:, port_total:].reshape(block_len, scen_rows, conv_count)
            * conv_drive[0, block_start : block_start + block_len],
            axis=(0, 1),
        )
        control_local = control_local + control_term
        fault_local = fault_local + fault_term
        received = jnp.stack(
            [
                passed_along(outbound[opposite[direction]], SUB, -offsets[direction])
                for direction in range(4)
            ]
        )
        window = jnp.concatenate(
            [received.reshape(4, slot_count, block_len, scen_rows), window[:, :, :block_len]],
            axis=2,
        )
    fault_local, control_local = sum_both(fault_local, control_local)
    return (adjoint_next[None], window[None], control_local[None], fault_local)


def solution(mesh):
    sub_mesh = Mesh(
        np.asarray(mesh.devices).reshape(SUB_SIZES + (mesh.shape["scen"],)), SUB + ("scen",)
    )
    return jax.shard_map(
        body,
        mesh=sub_mesh,
        in_specs=(
            P(SUB, None, None),
            P(None, SUB, "scen", None),
            P(SUB, "scen", None),
            P(SUB, None),
            P(SUB, None, None),
            P(SUB, None),
            P(SUB, None, None),
            P(SUB, None, None),
            P(SUB, None, None, None, "scen"),
            P(SUB, None),
            P(SUB, None, "scen", None),
            P("scen"),
            P(None, "scen"),
            P(None, "scen"),
        ),
        out_specs=(
            P(SUB, "scen", None),
            P(SUB, None, None, None, "scen"),
            P(SUB, None),
            P("scen"),
        ),
        check_vma=False,
    )
```

```python
import functools

import jax
import jax.numpy as jnp
import numpy as np
from jax.sharding import Mesh
from jax.experimental import pallas as pl
from jax.experimental.pallas import tpu as pltpu
from jax import lax
from jax.sharding import PartitionSpec as P

PRECISE = lax.Precision.HIGHEST


SUB = ("z_hi", "x", "y", "core")
SUB_SIZES = (2, 4, 8, 2)


def sum_both(fault_value, control_value):
    for axis in reversed(SUB[1:]):
        fault_value = lax.psum(fault_value, axis)
    fault_mask = (lax.iota(jnp.int32, lax.axis_size("scen")) == lax.axis_index("scen")).astype(
        jnp.float32
    )[:, None]
    control_mask = (lax.iota(jnp.int32, lax.axis_size(SUB[0])) == lax.axis_index(SUB[0])).astype(
        jnp.float32
    )[:, None]
    fault_slots, control_slots = lax.psum(
        (fault_mask * fault_value[None], control_mask * control_value[None]), (SUB[0], "scen")
    )
    return jnp.sum(fault_slots * fault_mask, axis=0), jnp.sum(control_slots * control_mask, axis=0)


def block_scan_kernel(
    block_start,
    grad_ref,
    picked_ref,
    spread_ref,
    companion_ref,
    start_ref,
    weights_ref,
    pick_ref,
    voltage_ref,
    last_ref,
    samples_ref,
    fault_out_ref,
    inflow_ref,
    adjoint_ref,
):
    steps, scen_rows, node_count = grad_ref.shape
    companion = companion_ref[...]
    inflow_ref[...] = jnp.dot(
        picked_ref[...], spread_ref[...], precision=lax.Precision.HIGH, preferred_element_type=jnp.float32
    )

    def one_step(index, adjoint_prev):
        step = steps - 1 - index
        rows = pl.ds(pl.multiple_of(step * scen_rows, scen_rows), scen_rows)
        right_side = (
            grad_ref[step].astype(jnp.float32)
            + companion * adjoint_prev
            + inflow_ref[rows]
        )
        adjoint = jnp.dot(
            right_side.astype(jnp.bfloat16), weights_ref[...], preferred_element_type=jnp.float32
        )
        adjoint_ref[rows] = adjoint
        return adjoint

    last_ref[...] = lax.fori_loop(0, steps, one_step, start_ref[...], unroll=True)
    adjoint_block = adjoint_ref[...]
    samples_ref[...] = jnp.dot(
        adjoint_block, pick_ref[...], precision=lax.Precision.HIGH, preferred_element_type=jnp.float32
    )
    fault_table = spread_ref[pl.ds(spread_ref.shape[0] - scen_rows, scen_rows), :]
    at_fault = jnp.sum(adjoint_block.reshape(steps, scen_rows, node_count) * fault_table[None], axis=2)
    voltage = voltage_ref[pl.ds(block_start, steps), :]
    fault_out_ref[...] = jnp.sum(at_fault * voltage, axis=0, keepdims=True)


def whole(array):
    return pl.BlockSpec(array.shape, lambda index: (0,) * array.ndim)


def block_scan(block_start, steps, grad, picked, spread, companion, start, weights, pick, voltage):
    _, _, scen_rows, node_count = grad.shape
    block_id = block_start // steps
    operands = (grad, picked, spread, companion, start, weights, pick, voltage)
    return pl.pallas_call(
        functools.partial(block_scan_kernel, block_start),
        grid=(1,),
        in_specs=[
            pl.BlockSpec(
                (steps, None, scen_rows, node_count), lambda index: (block_id, 0, 0, 0)
            )
        ]
        + [whole(array) for array in operands[1:]],
        out_specs=(
            whole(start),
            pl.BlockSpec((steps * scen_rows, pick.shape[1]), lambda index: (0, 0)),
            pl.BlockSpec((1, scen_rows), lambda index: (0, 0)),
        ),
        out_shape=(
            jax.ShapeDtypeStruct(start.shape, jnp.float32),
            jax.ShapeDtypeStruct((steps * scen_rows, pick.shape[1]), jnp.float32),
            jax.ShapeDtypeStruct((1, scen_rows), jnp.float32),
        ),
        scratch_shapes=[
            pltpu.VMEM((steps * scen_rows, node_count), jnp.float32),
            pltpu.VMEM((steps * scen_rows, node_count), jnp.float32),
        ],
    )(*operands)


def passed_along(value, axis, steps):
    count = lax.axis_size(axis)
    pairs = [(source, (source + steps) % count) for source in range(count)]
    return lax.ppermute(value, axis, pairs)


def body(
    inverse_matrix,
    objective_grad,
    final_adjoint,
    companion,
    port_node,
    line_count,
    line_delay,
    line_admittance,
    later_history,
    conv_node,
    conv_drive,
    fault_bus,
    fault_current,
    fault_voltage,
):
    node_count = inverse_matrix.shape[1]
    scen_rows = objective_grad.shape[2]
    slot_count = port_node.shape[2]
    port_total = 4 * slot_count
    conv_count = conv_node.shape[1]
    block_len = later_history.shape[3] // 2
    blocks = objective_grad.shape[0] // block_len
    sub_count = lax.axis_size(SUB)
    grid_width = max(2, sub_count // 16)
    offsets = (1, -1, grid_width, -grid_width)
    opposite = (1, 0, 3, 2)
    sub_index = lax.axis_index(SUB)
    weights = inverse_matrix[0]
    live_mask = (lax.iota(jnp.int32, slot_count)[None, :] < line_count[0][:, None]).astype(
        jnp.float32
    )
    node_iota = lax.iota(jnp.int32, node_count)
    pick_table = jnp.concatenate(
        [
            node_iota[:, None] == port_node[0].reshape(port_total)[None, :],
            node_iota[:, None] == conv_node[0][None, :],
        ],
        axis=1,
    ).astype(jnp.float32)
    line_scale = (line_admittance[0] * live_mask).reshape(port_total)
    fault_table = (node_iota[None, :] == (fault_bus - sub_index * node_count)[:, None]).astype(
        jnp.float32
    )
    spread_table = jnp.concatenate(
        [
            (port_node[0].reshape(port_total)[:, None] == node_iota[None, :]).astype(jnp.float32),
            fault_table,
        ],
        axis=0,
    )
    scen_eye = (lax.iota(jnp.int32, scen_rows)[:, None] == lax.iota(jnp.int32, scen_rows)[None, :]).astype(
        jnp.float32
    )
    window = later_history[0]
    adjoint_next = final_adjoint[0]
    control_local = jnp.zeros((conv_count,), jnp.float32)
    fault_local = jnp.zeros((scen_rows,), jnp.float32)
    block_rows = lax.iota(jnp.int32, block_len)
    time_iota = lax.iota(jnp.int32, 2 * block_len)


    for block_id in reversed(range(blocks)):
        block_start = block_id * block_len
        target = block_rows[None, None, :] + line_delay[0][:, :, None] - block_len
        time_table = (target[..., None] == time_iota).astype(jnp.float32)
        picked = jnp.concatenate(
            [
                jnp.einsum("ecji,ecis->jsec", time_table, window, precision=lax.Precision.HIGH).reshape(
                    block_len * scen_rows, port_total
                )
                * line_scale[None, :],
                (fault_current[block_start : block_start + block_len, :, None] * scen_eye[None]).reshape(
                    block_len * scen_rows, scen_rows
                ),
            ],
            axis=1,
        )
        adjoint_next, samples, fault_term = block_scan(
            block_start,
            block_len,
            objective_grad,
            picked,
            spread_table,
            companion,
            adjoint_next,
            weights,
            pick_table,
            fault_voltage,
        )
        samples, fault_term = lax.optimization_barrier((samples, fault_term[0]))
        series = (
            jnp.transpose(
                samples[:, :port_total].reshape(block_len, scen_rows, 4, slot_count), (2, 3, 0, 1)
            )
            * live_mask[:, :, None, None]
        )
        outbound = series.reshape(4, slot_count, block_len * scen_rows)
        control_term = jnp.sum(
            samples[:, port_total:].reshape(block_len, scen_rows, conv_count)
            * conv_drive[0, block_start : block_start + block_len],
            axis=(0, 1),
        )
        control_local = control_local + control_term
        fault_local = fault_local + fault_term
        received = jnp.stack(
            [
                passed_along(outbound[opposite[direction]], SUB, -offsets[direction])
                for direction in range(4)
            ]
        )
        window = jnp.concatenate(
            [received.reshape(4, slot_count, block_len, scen_rows), window[:, :, :block_len]],
            axis=2,
        )
    fault_local, control_local = sum_both(fault_local, control_local)
    return (adjoint_next[None], window[None], control_local[None], fault_local)


def solution(mesh):
    sub_mesh = Mesh(
        np.asarray(mesh.devices).reshape(SUB_SIZES + (mesh.shape["scen"],)), SUB + ("scen",)
    )
    return jax.shard_map(
        body,
        mesh=sub_mesh,
        in_specs=(
            P(SUB, None, None),
            P(None, SUB, "scen", None),
            P(SUB, "scen", None),
            P(SUB, None),
            P(SUB, None, None),
            P(SUB, None),
            P(SUB, None, None),
            P(SUB, None, None),
            P(SUB, None, None, None, "scen"),
            P(SUB, None),
            P(SUB, None, "scen", None),
            P("scen"),
            P(None, "scen"),
            P(None, "scen"),
        ),
        out_specs=(
            P(SUB, "scen", None),
            P(SUB, None, None, None, "scen"),
            P(SUB, None),
            P("scen"),
        ),
        check_vma=False,
    )
```

```python
import functools

import jax
import jax.numpy as jnp
import numpy as np
from jax.sharding import Mesh
from jax.experimental import pallas as pl
from jax.experimental.pallas import tpu as pltpu
from jax import lax
from jax.sharding import PartitionSpec as P

PRECISE = lax.Precision.HIGHEST


SUB = ("z_hi", "x", "y", "core")
SUB_SIZES = (2, 4, 8, 2)


def sum_both(fault_value, control_value):
    for axis in reversed(SUB[1:]):
        fault_value = lax.psum(fault_value, axis)
    fault_mask = (lax.iota(jnp.int32, lax.axis_size("scen")) == lax.axis_index("scen")).astype(
        jnp.float32
    )[:, None]
    control_mask = (lax.iota(jnp.int32, lax.axis_size(SUB[0])) == lax.axis_index(SUB[0])).astype(
        jnp.float32
    )[:, None]
    fault_slots, control_slots = lax.psum(
        (fault_mask * fault_value[None], control_mask * control_value[None]), (SUB[0], "scen")
    )
    return jnp.sum(fault_slots * fault_mask, axis=0), jnp.sum(control_slots * control_mask, axis=0)


def block_scan_kernel(
    block_start,
    grad_ref,
    picked_ref,
    spread_ref,
    companion_ref,
    start_ref,
    weights_ref,
    pick_ref,
    voltage_ref,
    last_ref,
    samples_ref,
    fault_out_ref,
    inflow_ref,
    adjoint_ref,
):
    steps, scen_rows, node_count = grad_ref.shape
    companion = companion_ref[...]
    inflow_ref[...] = jnp.dot(
        picked_ref[...], spread_ref[...], precision=lax.Precision.HIGH, preferred_element_type=jnp.float32
    )

    def one_step(index, adjoint_prev):
        step = steps - 1 - index
        rows = pl.ds(pl.multiple_of(step * scen_rows, scen_rows), scen_rows)
        right_side = (
            grad_ref[step].astype(jnp.float32)
            + companion * adjoint_prev
            + inflow_ref[rows]
        )
        adjoint = jnp.dot(
            right_side.astype(jnp.bfloat16), weights_ref[...], preferred_element_type=jnp.float32
        )
        adjoint_ref[rows] = adjoint
        return adjoint

    last_ref[...] = lax.fori_loop(0, steps, one_step, start_ref[...], unroll=True)
    adjoint_block = adjoint_ref[...]
    picks = jnp.dot(
        adjoint_block, pick_ref[...], precision=lax.Precision.HIGH, preferred_element_type=jnp.float32
    )
    sample_count = samples_ref.shape[1]
    samples_ref[...] = picks[:, :sample_count]
    at_fault = picks[:, sample_count:].reshape(steps, scen_rows, scen_rows)
    own = (
        lax.broadcasted_iota(jnp.int32, (scen_rows, scen_rows), 0)
        == lax.broadcasted_iota(jnp.int32, (scen_rows, scen_rows), 1)
    ).astype(jnp.float32)
    voltage = voltage_ref[pl.ds(block_start, steps), :]
    fault_out_ref[...] = jnp.sum(
        jnp.sum(at_fault * own[None] * voltage[:, None, :], axis=0), axis=0, keepdims=True
    )


def whole(array):
    return pl.BlockSpec(array.shape, lambda index: (0,) * array.ndim)


def block_scan(block_start, steps, grad, picked, spread, companion, start, weights, pick, voltage):
    _, _, scen_rows, node_count = grad.shape
    block_id = block_start // steps
    operands = (grad, picked, spread, companion, start, weights, pick, voltage)
    return pl.pallas_call(
        functools.partial(block_scan_kernel, block_start),
        grid=(1,),
        in_specs=[
            pl.BlockSpec(
                (steps, None, scen_rows, node_count), lambda index: (block_id, 0, 0, 0)
            )
        ]
        + [whole(array) for array in operands[1:]],
        out_specs=(
            whole(start),
            pl.BlockSpec((steps * scen_rows, pick.shape[1] - scen_rows), lambda index: (0, 0)),
            pl.BlockSpec((1, scen_rows), lambda index: (0, 0)),
        ),
        out_shape=(
            jax.ShapeDtypeStruct(start.shape, jnp.float32),
            jax.ShapeDtypeStruct((steps * scen_rows, pick.shape[1] - scen_rows), jnp.float32),
            jax.ShapeDtypeStruct((1, scen_rows), jnp.float32),
        ),
        scratch_shapes=[
            pltpu.VMEM((steps * scen_rows, node_count), jnp.float32),
            pltpu.VMEM((steps * scen_rows, node_count), jnp.float32),
        ],
    )(*operands)


def passed_along(value, axis, steps):
    count = lax.axis_size(axis)
    pairs = [(source, (source + steps) % count) for source in range(count)]
    return lax.ppermute(value, axis, pairs)


def body(
    inverse_matrix,
    objective_grad,
    final_adjoint,
    companion,
    port_node,
    line_count,
    line_delay,
    line_admittance,
    later_history,
    conv_node,
    conv_drive,
    fault_bus,
    fault_current,
    fault_voltage,
):
    node_count = inverse_matrix.shape[1]
    scen_rows = objective_grad.shape[2]
    slot_count = port_node.shape[2]
    port_total = 4 * slot_count
    conv_count = conv_node.shape[1]
    block_len = later_history.shape[3] // 2
    blocks = objective_grad.shape[0] // block_len
    sub_count = lax.axis_size(SUB)
    grid_width = max(2, sub_count // 16)
    offsets = (1, -1, grid_width, -grid_width)
    opposite = (1, 0, 3, 2)
    sub_index = lax.axis_index(SUB)
    weights = inverse_matrix[0]
    live_mask = (lax.iota(jnp.int32, slot_count)[None, :] < line_count[0][:, None]).astype(
        jnp.float32
    )
    node_iota = lax.iota(jnp.int32, node_count)
    pick_table = jnp.concatenate(
        [
            node_iota[:, None] == port_node[0].reshape(port_total)[None, :],
            node_iota[:, None] == conv_node[0][None, :],
            node_iota[:, None] == (fault_bus - sub_index * node_count)[None, :],
        ],
        axis=1,
    ).astype(jnp.float32)
    line_scale = (line_admittance[0] * live_mask).reshape(port_total)
    fault_table = (node_iota[None, :] == (fault_bus - sub_index * node_count)[:, None]).astype(
        jnp.float32
    )
    spread_table = jnp.concatenate(
        [
            (port_node[0].reshape(port_total)[:, None] == node_iota[None, :]).astype(jnp.float32),
            fault_table,
        ],
        axis=0,
    )
    scen_eye = (lax.iota(jnp.int32, scen_rows)[:, None] == lax.iota(jnp.int32, scen_rows)[None, :]).astype(
        jnp.float32
    )
    window = later_history[0]
    adjoint_next = final_adjoint[0]
    control_local = jnp.zeros((conv_count,), jnp.float32)
    fault_local = jnp.zeros((scen_rows,), jnp.float32)
    block_rows = lax.iota(jnp.int32, block_len)
    time_iota = lax.iota(jnp.int32, 2 * block_len)


    for block_id in reversed(range(blocks)):
        block_start = block_id * block_len
        target = block_rows[None, None, :] + line_delay[0][:, :, None] - block_len
        time_table = (target[..., None] == time_iota).astype(jnp.float32)
        picked = jnp.concatenate(
            [
                jnp.einsum("ecji,ecis->jsec", time_table, window, precision=lax.Precision.HIGH).reshape(
                    block_len * scen_rows, port_total
                )
                * line_scale[None, :],
                (fault_current[block_start : block_start + block_len, :, None] * scen_eye[None]).reshape(
                    block_len * scen_rows, scen_rows
                ),
            ],
            axis=1,
        )
        adjoint_next, samples, fault_term = block_scan(
            block_start,
            block_len,
            objective_grad,
            picked,
            spread_table,
            companion,
            adjoint_next,
            weights,
            pick_table,
            fault_voltage,
        )
        samples, fault_term = lax.optimization_barrier((samples, fault_term[0]))
        series = (
            jnp.transpose(
                samples[:, :port_total].reshape(block_len, scen_rows, 4, slot_count), (2, 3, 0, 1)
            )
            * live_mask[:, :, None, None]
        )
        outbound = series.reshape(4, slot_count, block_len * scen_rows)
        control_term = jnp.sum(
            samples[:, port_total:].reshape(block_len, scen_rows, conv_count)
            * conv_drive[0, block_start : block_start + block_len],
            axis=(0, 1),
        )
        control_local = control_local + control_term
        fault_local = fault_local + fault_term
        received = jnp.stack(
            [
                passed_along(outbound[opposite[direction]], SUB, -offsets[direction])
                for direction in range(4)
            ]
        )
        window = jnp.concatenate(
            [received.reshape(4, slot_count, block_len, scen_rows), window[:, :, :block_len]],
            axis=2,
        )
    fault_local, control_local = sum_both(fault_local, control_local)
    return (adjoint_next[None], window[None], control_local[None], fault_local)


def solution(mesh):
    sub_mesh = Mesh(
        np.asarray(mesh.devices).reshape(SUB_SIZES + (mesh.shape["scen"],)), SUB + ("scen",)
    )
    return jax.shard_map(
        body,
        mesh=sub_mesh,
        in_specs=(
            P(SUB, None, None),
            P(None, SUB, "scen", None),
            P(SUB, "scen", None),
            P(SUB, None),
            P(SUB, None, None),
            P(SUB, None),
            P(SUB, None, None),
            P(SUB, None, None),
            P(SUB, None, None, None, "scen"),
            P(SUB, None),
            P(SUB, None, "scen", None),
            P("scen"),
            P(None, "scen"),
            P(None, "scen"),
        ),
        out_specs=(
            P(SUB, "scen", None),
            P(SUB, None, None, None, "scen"),
            P(SUB, None),
            P("scen"),
        ),
        check_vma=False,
    )
```

```python
import functools

import jax
import jax.numpy as jnp
import numpy as np
from jax.sharding import Mesh
from jax.experimental import pallas as pl
from jax.experimental.pallas import tpu as pltpu
from jax import lax
from jax.sharding import PartitionSpec as P

PRECISE = lax.Precision.HIGHEST


SUB = ("z_hi", "x", "y", "core")
SUB_SIZES = (2, 4, 8, 2)


def sum_both(fault_value, control_value):
    for axis in reversed(SUB[1:]):
        fault_value = lax.psum(fault_value, axis)
    fault_mask = (lax.iota(jnp.int32, lax.axis_size("scen")) == lax.axis_index("scen")).astype(
        jnp.float32
    )[:, None]
    control_mask = (lax.iota(jnp.int32, lax.axis_size(SUB[0])) == lax.axis_index(SUB[0])).astype(
        jnp.float32
    )[:, None]
    fault_slots, control_slots = lax.psum(
        (fault_mask * fault_value[None], control_mask * control_value[None]), (SUB[0], "scen")
    )
    return jnp.sum(fault_slots * fault_mask, axis=0), jnp.sum(control_slots * control_mask, axis=0)


def block_scan_kernel(
    block_start,
    grad_ref,
    picked_ref,
    spread_ref,
    companion_ref,
    start_ref,
    weights_ref,
    pick_ref,
    voltage_ref,
    last_ref,
    samples_ref,
    fault_out_ref,
    inflow_ref,
    adjoint_ref,
    weights_vmem,
    weights_arrived,
):
    steps, scen_rows, node_count = grad_ref.shape
    companion = companion_ref[...]
    weights_copy = pltpu.make_async_copy(weights_ref, weights_vmem, weights_arrived)
    weights_copy.start()
    inflow_ref[...] = jnp.dot(
        picked_ref[...], spread_ref[...], precision=lax.Precision.HIGH, preferred_element_type=jnp.float32
    )

    weights_copy.wait()

    def one_step(index, adjoint_prev):
        step = steps - 1 - index
        rows = pl.ds(pl.multiple_of(step * scen_rows, scen_rows), scen_rows)
        right_side = (
            grad_ref[step].astype(jnp.float32)
            + companion * adjoint_prev
            + inflow_ref[rows]
        )
        adjoint = jnp.dot(
            right_side.astype(jnp.bfloat16), weights_vmem[...], preferred_element_type=jnp.float32
        )
        adjoint_ref[rows] = adjoint
        return adjoint

    last_ref[...] = lax.fori_loop(0, steps, one_step, start_ref[...], unroll=True)
    adjoint_block = adjoint_ref[...]
    samples_ref[...] = jnp.dot(
        adjoint_block, pick_ref[...], precision=lax.Precision.HIGH, preferred_element_type=jnp.float32
    )
    fault_table = spread_ref[pl.ds(spread_ref.shape[0] - scen_rows, scen_rows), :]
    at_fault = jnp.sum(adjoint_block.reshape(steps, scen_rows, node_count) * fault_table[None], axis=2)
    voltage = voltage_ref[pl.ds(block_start, steps), :]
    fault_out_ref[...] = jnp.sum(at_fault * voltage, axis=0, keepdims=True)


def whole(array):
    return pl.BlockSpec(array.shape, lambda index: (0,) * array.ndim)


def block_scan(block_start, steps, grad, picked, spread, companion, start, weights, pick, voltage):
    _, _, scen_rows, node_count = grad.shape
    block_id = block_start // steps
    operands = (grad, picked, spread, companion, start, weights, pick, voltage)
    return pl.pallas_call(
        functools.partial(block_scan_kernel, block_start),
        grid=(1,),
        in_specs=[
            pl.BlockSpec(
                (steps, None, scen_rows, node_count), lambda index: (block_id, 0, 0, 0)
            )
        ]
        + [
            pl.BlockSpec(memory_space=pl.ANY) if array is weights else whole(array)
            for array in operands[1:]
        ],
        out_specs=(
            whole(start),
            pl.BlockSpec((steps * scen_rows, pick.shape[1]), lambda index: (0, 0)),
            pl.BlockSpec((1, scen_rows), lambda index: (0, 0)),
        ),
        out_shape=(
            jax.ShapeDtypeStruct(start.shape, jnp.float32),
            jax.ShapeDtypeStruct((steps * scen_rows, pick.shape[1]), jnp.float32),
            jax.ShapeDtypeStruct((1, scen_rows), jnp.float32),
        ),
        scratch_shapes=[
            pltpu.VMEM((steps * scen_rows, node_count), jnp.float32),
            pltpu.VMEM((steps * scen_rows, node_count), jnp.float32),
            pltpu.VMEM(weights.shape, weights.dtype),
            pltpu.SemaphoreType.DMA,
        ],
    )(*operands)


def passed_along(value, axis, steps):
    count = lax.axis_size(axis)
    pairs = [(source, (source + steps) % count) for source in range(count)]
    return lax.ppermute(value, axis, pairs)


def body(
    inverse_matrix,
    objective_grad,
    final_adjoint,
    companion,
    port_node,
    line_count,
    line_delay,
    line_admittance,
    later_history,
    conv_node,
    conv_drive,
    fault_bus,
    fault_current,
    fault_voltage,
):
    node_count = inverse_matrix.shape[1]
    scen_rows = objective_grad.shape[2]
    slot_count = port_node.shape[2]
    port_total = 4 * slot_count
    conv_count = conv_node.shape[1]
    block_len = later_history.shape[3] // 2
    blocks = objective_grad.shape[0] // block_len
    sub_count = lax.axis_size(SUB)
    grid_width = max(2, sub_count // 16)
    offsets = (1, -1, grid_width, -grid_width)
    opposite = (1, 0, 3, 2)
    sub_index = lax.axis_index(SUB)
    weights = inverse_matrix[0]
    live_mask = (lax.iota(jnp.int32, slot_count)[None, :] < line_count[0][:, None]).astype(
        jnp.float32
    )
    node_iota = lax.iota(jnp.int32, node_count)
    pick_table = jnp.concatenate(
        [
            node_iota[:, None] == port_node[0].reshape(port_total)[None, :],
            node_iota[:, None] == conv_node[0][None, :],
        ],
        axis=1,
    ).astype(jnp.float32)
    line_scale = (line_admittance[0] * live_mask).reshape(port_total)
    fault_table = (node_iota[None, :] == (fault_bus - sub_index * node_count)[:, None]).astype(
        jnp.float32
    )
    spread_table = jnp.concatenate(
        [
            (port_node[0].reshape(port_total)[:, None] == node_iota[None, :]).astype(jnp.float32),
            fault_table,
        ],
        axis=0,
    )
    scen_eye = (lax.iota(jnp.int32, scen_rows)[:, None] == lax.iota(jnp.int32, scen_rows)[None, :]).astype(
        jnp.float32
    )
    window = later_history[0]
    adjoint_next = final_adjoint[0]
    control_local = jnp.zeros((conv_count,), jnp.float32)
    fault_local = jnp.zeros((scen_rows,), jnp.float32)
    block_rows = lax.iota(jnp.int32, block_len)
    time_iota = lax.iota(jnp.int32, 2 * block_len)


    for block_id in reversed(range(blocks)):
        block_start = block_id * block_len
        target = block_rows[None, None, :] + line_delay[0][:, :, None] - block_len
        time_table = (target[..., None] == time_iota).astype(jnp.float32)
        picked = jnp.concatenate(
            [
                jnp.einsum("ecji,ecis->jsec", time_table, window, precision=lax.Precision.HIGH).reshape(
                    block_len * scen_rows, port_total
                )
                * line_scale[None, :],
                (fault_current[block_start : block_start + block_len, :, None] * scen_eye[None]).reshape(
                    block_len * scen_rows, scen_rows
                ),
            ],
            axis=1,
        )
        adjoint_next, samples, fault_term = block_scan(
            block_start,
            block_len,
            objective_grad,
            picked,
            spread_table,
            companion,
            adjoint_next,
            weights,
            pick_table,
            fault_voltage,
        )
        samples, fault_term = lax.optimization_barrier((samples, fault_term[0]))
        series = (
            jnp.transpose(
                samples[:, :port_total].reshape(block_len, scen_rows, 4, slot_count), (2, 3, 0, 1)
            )
            * live_mask[:, :, None, None]
        )
        outbound = series.reshape(4, slot_count, block_len * scen_rows)
        control_term = jnp.sum(
            samples[:, port_total:].reshape(block_len, scen_rows, conv_count)
            * conv_drive[0, block_start : block_start + block_len],
            axis=(0, 1),
        )
        control_local = control_local + control_term
        fault_local = fault_local + fault_term
        received = jnp.stack(
            [
                passed_along(outbound[opposite[direction]], SUB, -offsets[direction])
                for direction in range(4)
            ]
        )
        window = jnp.concatenate(
            [received.reshape(4, slot_count, block_len, scen_rows), window[:, :, :block_len]],
            axis=2,
        )
    fault_local, control_local = sum_both(fault_local, control_local)
    return (adjoint_next[None], window[None], control_local[None], fault_local)


def solution(mesh):
    sub_mesh = Mesh(
        np.asarray(mesh.devices).reshape(SUB_SIZES + (mesh.shape["scen"],)), SUB + ("scen",)
    )
    return jax.shard_map(
        body,
        mesh=sub_mesh,
        in_specs=(
            P(SUB, None, None),
            P(None, SUB, "scen", None),
            P(SUB, "scen", None),
            P(SUB, None),
            P(SUB, None, None),
            P(SUB, None),
            P(SUB, None, None),
            P(SUB, None, None),
            P(SUB, None, None, None, "scen"),
            P(SUB, None),
            P(SUB, None, "scen", None),
            P("scen"),
            P(None, "scen"),
            P(None, "scen"),
        ),
        out_specs=(
            P(SUB, "scen", None),
            P(SUB, None, None, None, "scen"),
            P(SUB, None),
            P("scen"),
        ),
        check_vma=False,
    )
```

```python
import functools

import jax
import jax.numpy as jnp
import numpy as np
from jax.sharding import Mesh
from jax.experimental import pallas as pl
from jax.experimental.pallas import tpu as pltpu
from jax import lax
from jax.sharding import PartitionSpec as P

PRECISE = lax.Precision.HIGHEST


SUB = ("z_hi", "x", "y", "core")
SUB_SIZES = (2, 4, 8, 2)


def sum_both(fault_value, control_value):
    for axis in reversed(SUB[1:]):
        fault_value = lax.psum(fault_value, axis)
    fault_mask = (lax.iota(jnp.int32, lax.axis_size("scen")) == lax.axis_index("scen")).astype(
        jnp.float32
    )[:, None]
    control_mask = (lax.iota(jnp.int32, lax.axis_size(SUB[0])) == lax.axis_index(SUB[0])).astype(
        jnp.float32
    )[:, None]
    fault_slots, control_slots = lax.psum(
        (fault_mask * fault_value[None], control_mask * control_value[None]), (SUB[0], "scen")
    )
    return jnp.sum(fault_slots * fault_mask, axis=0), jnp.sum(control_slots * control_mask, axis=0)


def block_scan_kernel(
    block_start,
    grad_ref,
    picked_ref,
    spread_ref,
    companion_ref,
    start_ref,
    weights_ref,
    pick_ref,
    voltage_ref,
    last_ref,
    samples_ref,
    fault_out_ref,
    inflow_ref,
    adjoint_ref,
):
    steps, scen_rows, node_count = grad_ref.shape
    companion = companion_ref[...]
    inflow_ref[...] = jnp.dot(
        picked_ref[...], spread_ref[...], preferred_element_type=jnp.float32
    )

    def one_step(index, adjoint_prev):
        step = steps - 1 - index
        rows = pl.ds(pl.multiple_of(step * scen_rows, scen_rows), scen_rows)
        right_side = (
            grad_ref[step].astype(jnp.float32)
            + companion * adjoint_prev
            + inflow_ref[rows]
        )
        adjoint = jnp.dot(
            right_side.astype(jnp.bfloat16), weights_ref[...], preferred_element_type=jnp.float32
        )
        adjoint_ref[rows] = adjoint
        return adjoint

    last_ref[...] = lax.fori_loop(0, steps, one_step, start_ref[...], unroll=True)
    adjoint_block = adjoint_ref[...]
    samples_ref[...] = jnp.dot(
        adjoint_block, pick_ref[...], precision=lax.Precision.HIGH, preferred_element_type=jnp.float32
    )
    fault_table = spread_ref[pl.ds(spread_ref.shape[0] - scen_rows, scen_rows), :]
    at_fault = jnp.sum(adjoint_block.reshape(steps, scen_rows, node_count) * fault_table[None], axis=2)
    voltage = voltage_ref[pl.ds(block_start, steps), :]
    fault_out_ref[...] = jnp.sum(at_fault * voltage, axis=0, keepdims=True)


def whole(array):
    return pl.BlockSpec(array.shape, lambda index: (0,) * array.ndim)


def block_scan(block_start, steps, grad, picked, spread, companion, start, weights, pick, voltage):
    _, _, scen_rows, node_count = grad.shape
    block_id = block_start // steps
    operands = (grad, picked, spread, companion, start, weights, pick, voltage)
    return pl.pallas_call(
        functools.partial(block_scan_kernel, block_start),
        grid=(1,),
        in_specs=[
            pl.BlockSpec(
                (steps, None, scen_rows, node_count), lambda index: (block_id, 0, 0, 0)
            )
        ]
        + [whole(array) for array in operands[1:]],
        out_specs=(
            whole(start),
            pl.BlockSpec((steps * scen_rows, pick.shape[1]), lambda index: (0, 0)),
            pl.BlockSpec((1, scen_rows), lambda index: (0, 0)),
        ),
        out_shape=(
            jax.ShapeDtypeStruct(start.shape, jnp.float32),
            jax.ShapeDtypeStruct((steps * scen_rows, pick.shape[1]), jnp.float32),
            jax.ShapeDtypeStruct((1, scen_rows), jnp.float32),
        ),
        scratch_shapes=[
            pltpu.VMEM((steps * scen_rows, node_count), jnp.float32),
            pltpu.VMEM((steps * scen_rows, node_count), jnp.float32),
        ],
    )(*operands)


def passed_along(value, axis, steps):
    count = lax.axis_size(axis)
    pairs = [(source, (source + steps) % count) for source in range(count)]
    return lax.ppermute(value, axis, pairs)


def body(
    inverse_matrix,
    objective_grad,
    final_adjoint,
    companion,
    port_node,
    line_count,
    line_delay,
    line_admittance,
    later_history,
    conv_node,
    conv_drive,
    fault_bus,
    fault_current,
    fault_voltage,
):
    node_count = inverse_matrix.shape[1]
    scen_rows = objective_grad.shape[2]
    slot_count = port_node.shape[2]
    port_total = 4 * slot_count
    conv_count = conv_node.shape[1]
    block_len = later_history.shape[3] // 2
    blocks = objective_grad.shape[0] // block_len
    sub_count = lax.axis_size(SUB)
    grid_width = max(2, sub_count // 16)
    offsets = (1, -1, grid_width, -grid_width)
    opposite = (1, 0, 3, 2)
    sub_index = lax.axis_index(SUB)
    weights = inverse_matrix[0]
    live_mask = (lax.iota(jnp.int32, slot_count)[None, :] < line_count[0][:, None]).astype(
        jnp.float32
    )
    node_iota = lax.iota(jnp.int32, node_count)
    pick_table = jnp.concatenate(
        [
            node_iota[:, None] == port_node[0].reshape(port_total)[None, :],
            node_iota[:, None] == conv_node[0][None, :],
        ],
        axis=1,
    ).astype(jnp.float32)
    line_scale = (line_admittance[0] * live_mask).reshape(port_total)
    fault_table = (node_iota[None, :] == (fault_bus - sub_index * node_count)[:, None]).astype(
        jnp.float32
    )
    spread_table = jnp.concatenate(
        [
            (port_node[0].reshape(port_total)[:, None] == node_iota[None, :]).astype(jnp.float32),
            fault_table,
        ],
        axis=0,
    )
    scen_eye = (lax.iota(jnp.int32, scen_rows)[:, None] == lax.iota(jnp.int32, scen_rows)[None, :]).astype(
        jnp.float32
    )
    window = later_history[0]
    adjoint_next = final_adjoint[0]
    control_local = jnp.zeros((conv_count,), jnp.float32)
    fault_local = jnp.zeros((scen_rows,), jnp.float32)
    block_rows = lax.iota(jnp.int32, block_len)
    time_iota = lax.iota(jnp.int32, 2 * block_len)


    for block_id in reversed(range(blocks)):
        block_start = block_id * block_len
        target = block_rows[None, None, :] + line_delay[0][:, :, None] - block_len
        time_table = (target[..., None] == time_iota).astype(jnp.float32)
        picked = jnp.concatenate(
            [
                jnp.einsum("ecji,ecis->jsec", time_table, window, precision=lax.Precision.HIGH).reshape(
                    block_len * scen_rows, port_total
                )
                * line_scale[None, :],
                (fault_current[block_start : block_start + block_len, :, None] * scen_eye[None]).reshape(
                    block_len * scen_rows, scen_rows
                ),
            ],
            axis=1,
        )
        adjoint_next, samples, fault_term = block_scan(
            block_start,
            block_len,
            objective_grad,
            picked,
            spread_table,
            companion,
            adjoint_next,
            weights,
            pick_table,
            fault_voltage,
        )
        samples, fault_term = lax.optimization_barrier((samples, fault_term[0]))
        series = (
            jnp.transpose(
                samples[:, :port_total].reshape(block_len, scen_rows, 4, slot_count), (2, 3, 0, 1)
            )
            * live_mask[:, :, None, None]
        )
        outbound = series.reshape(4, slot_count, block_len * scen_rows)
        control_term = jnp.sum(
            samples[:, port_total:].reshape(block_len, scen_rows, conv_count)
            * conv_drive[0, block_start : block_start + block_len],
            axis=(0, 1),
        )
        control_local = control_local + control_term
        fault_local = fault_local + fault_term
        received = jnp.stack(
            [
                passed_along(outbound[opposite[direction]], SUB, -offsets[direction])
                for direction in range(4)
            ]
        )
        window = jnp.concatenate(
            [received.reshape(4, slot_count, block_len, scen_rows), window[:, :, :block_len]],
            axis=2,
        )
    fault_local, control_local = sum_both(fault_local, control_local)
    return (adjoint_next[None], window[None], control_local[None], fault_local)


def solution(mesh):
    sub_mesh = Mesh(
        np.asarray(mesh.devices).reshape(SUB_SIZES + (mesh.shape["scen"],)), SUB + ("scen",)
    )
    return jax.shard_map(
        body,
        mesh=sub_mesh,
        in_specs=(
            P(SUB, None, None),
            P(None, SUB, "scen", None),
            P(SUB, "scen", None),
            P(SUB, None),
            P(SUB, None, None),
            P(SUB, None),
            P(SUB, None, None),
            P(SUB, None, None),
            P(SUB, None, None, None, "scen"),
            P(SUB, None),
            P(SUB, None, "scen", None),
            P("scen"),
            P(None, "scen"),
            P(None, "scen"),
        ),
        out_specs=(
            P(SUB, "scen", None),
            P(SUB, None, None, None, "scen"),
            P(SUB, None),
            P("scen"),
        ),
        check_vma=False,
    )
```
